128 devices in a mesh: group: 8 (over y, core), member: 16 (over z, x).
Axes of the slice: x: 4, y: 4, z: 4, core: 2. Of those that a mesh axis runs over, the one named last changes fastest.
Arguments:
- candidates: bfloat16 [512, 64, 1024], P('member', 'group'), may hold values from -6 to 6
- kv_cache: bfloat16 [64, 2048, 2048], P('group', 'member'), may hold values from -6 to 6
- cache_request: int32 [64], replicated, may hold values from 0 to 63, as said below
- rank_request: int32 [64], replicated, may hold values from 0 to 63, as said below
- hist_blocks: int32 [64], replicated, may hold values from 1 to 16, 544 in all
- w_uq: bfloat16 [1024, 2048], replicated, may hold values from -0.1875 to 0.1875
- w_out: bfloat16 [1024, 1024], replicated, may hold values from -0.1875 to 0.1875
Outputs:
- ranked: bfloat16 [512, 64, 1024], P('member', 'group')
The draws below stay inside these ranges and needn't reach their ends.
Inputs may be any that keep to these rules, and one draw needn't show every extreme that they name: `cache_request`: A permutation; cache row q lies on group q // 8, events split over member. `rank_request`: A permutation; group g ranks positions g * 8 to (g + 1) * 8 - 1. The requests cached on one group are dealt out to the ranking groups in turn, so every pair of groups carries 8 // 8 or 1 requests and some pair carries exactly 1; the uneven part of the load is the live history lengths.
All inputs are finite; a program needn't handle non-finite values.
Results may differ from the reference program's by a relative error of at most 0.011.
Values may be sent and summed in bfloat16 or wider, within the bound.
No kernel may reach another device: no remote copies, remote signals or barrier semaphores. Data moves between devices by JAX's collectives and lax.ppermute only.
A program may use at most 320 MiB of HBM per device.

```python
import math
import jax
import jax.numpy as jnp
import numpy as np
from jax import lax

D = 1024
HEADS = 8
HEAD_DIM = 128
BLK = 128
HIST_BLOCKS = 16
HIST_EV = 2048
CANDS = 512
REQ_GRP = 8
REQUESTS = 64


def assignment(key):
    key = jax.random.fold_in(key, 7)
    key_one, key_two, key_three, key_four = jax.random.split(key, 4)
    groups = REQUESTS // REQ_GRP
    request_perm = jax.random.permutation(key_one, REQUESTS).astype(jnp.int32)
    group_perm = jax.random.permutation(key_two, groups).astype(jnp.int32)
    local_scores = jax.random.randint(key_three, (groups, REQ_GRP), 0, 4096) * REQ_GRP + jnp.arange(REQ_GRP)[None, :]
    local_rank = jnp.argsort(jnp.argsort(local_scores, axis=1), axis=1).astype(jnp.int32)
    slot_ids = jnp.arange(REQUESTS, dtype=jnp.int32)
    owner_grp = slot_ids // REQ_GRP
    ranker = group_perm[(owner_grp + local_rank.reshape(-1)) % groups]
    tie_break = jax.random.randint(key_four, (REQUESTS,), 0, 4096) * REQUESTS + slot_ids
    rank_slot = jnp.argsort(ranker * (4096 * REQUESTS) + tie_break)
    return (request_perm, request_perm[rank_slot].astype(jnp.int32))


def draw_cache_request(key, part):
    return assignment(key)[0]


def draw_rank_request(key, part):
    return assignment(key)[1]


def levels(stream_key, dims, cuts, smallest, largest):
    level = 1.0
    for axis_at, parts in cuts:
        heights = jax.random.uniform(jax.random.fold_in(jax.random.fold_in(stream_key, 6), axis_at), (parts,), jnp.float32, smallest / len(cuts), largest / len(cuts))
        level = level * jnp.repeat(jnp.exp(heights), dims[axis_at] // parts).reshape((-1,) + (1,) * (len(dims) - 1 - axis_at))
    return level


def split_up(number_of, total, bound, skew):
    loads = [(1 << 20) // math.isqrt(grade ** skew) + 1 for grade in range(2, number_of + 1)]
    spare, holding = total - bound - (number_of - 1), [1] * (number_of - 1)
    while spare > 0:
        free = [i for i in range(number_of - 1) if holding[i] < bound]
        whole, budget = sum([loads[i] for i in free]), spare
        for i in free:
            extra = min(bound - holding[i], max(1, budget * loads[i] // whole), spare)
            holding[i] = holding[i] + extra
            spare = spare - extra
    return np.array([bound] + holding)


def uneven_parts(rng, number_of, total, reach, skew):
    if number_of == 2:
        one = jax.random.randint(rng, (), max(1, total - reach), min(reach, total - 1) + 1)
        return jnp.stack([one, total - one])
    tallies = jnp.asarray(split_up(number_of, total, reach, skew), jnp.int32)
    pairs = (number_of - 1) // 2
    giver, taker = tallies[1:1 + 2 * pairs:2], tallies[2:2 + 2 * pairs:2]
    room = jnp.minimum(giver - 1, reach - taker)
    passed = jax.random.randint(jax.random.fold_in(rng, 1), (pairs,), 0, 1 << 20) % (room + 1)
    tallies = tallies.at[1:1 + 2 * pairs:2].set(giver - passed).at[2:2 + 2 * pairs:2].set(taker + passed)
    return tallies[jax.random.permutation(jax.random.fold_in(rng, 2), number_of)]


def gaussian(stream_key, extent, deviation, bound, cuts=(), kind=jnp.bfloat16):
    entries = deviation * jax.random.normal(stream_key, extent, jnp.float32)
    if cuts:
        entries = entries * levels(stream_key, extent, cuts, -0.22, 0.18)
    return jnp.clip(entries, -bound, bound).astype(kind)


def setup_inputs(seed: int = 0) -> dict:
    splits = jax.random.split(jax.random.key(seed), 8)
    candidates = gaussian(splits[0], (CANDS, REQUESTS, D), 1.0, 6.0, ((0, 16), (1, 8)))
    kv_cache = gaussian(splits[1], (REQUESTS, HIST_EV, 2 * D), 1.0, 6.0, ((0, 8), (1, 16)))
    cache_request = draw_cache_request(jax.random.fold_in(splits[7], 71), 0)
    rank_request = draw_rank_request(jax.random.fold_in(splits[7], 71), 0)
    hist_blocks = uneven_parts(splits[4], REQUESTS, REQUESTS * (HIST_BLOCKS + 1) // 2, HIST_BLOCKS, 2).astype(jnp.int32)
    w_uq = gaussian(splits[5], (D, 2 * D), D ** -0.5, 0.1875)
    w_out = gaussian(splits[6], (D, D), D ** -0.5, 0.1875)
    return dict(candidates=candidates, kv_cache=kv_cache, cache_request=cache_request, rank_request=rank_request, hist_blocks=hist_blocks, w_uq=w_uq, w_out=w_out)


def layer_norm(values):
    center = values - lax.optimization_barrier(jnp.mean(values, axis=-1, keepdims=True))
    spread = lax.optimization_barrier(jnp.mean(center * center, axis=-1, keepdims=True))
    return center * lax.rsqrt(spread + 1e-05)

def reference(candidates, kv_cache, cache_request, rank_request, hist_blocks, w_uq, w_out):
    slot_ids = jnp.arange(REQUESTS, dtype=jnp.int32)
    match = cache_request[:, None] == rank_request[None, :]
    slot_of_pos = lax.optimization_barrier(jnp.sum(jnp.where(match, slot_ids[:, None], 0), axis=0)).astype(jnp.int32)
    live = (hist_blocks[rank_request] * BLK).astype(jnp.float32)
    inputs = candidates.astype(jnp.float32)
    normed = layer_norm(inputs).astype(jnp.bfloat16).reshape(CANDS * REQUESTS, D)
    projected = jax.nn.silu(jnp.dot(normed, w_uq, preferred_element_type=jnp.float32))
    gates = projected[:, :D].reshape(CANDS, REQUESTS, D)
    queries = projected[:, D:].astype(jnp.bfloat16).reshape(CANDS, REQUESTS, HEADS, HEAD_DIM)
    scale = HEAD_DIM ** (-0.5)
    events = jnp.arange(HIST_EV).astype(jnp.float32)

    def one_request(position):
        panel = kv_cache[slot_of_pos[position]].astype(jnp.float32)
        keys = panel[:, :D].reshape(HIST_EV, HEADS, HEAD_DIM)
        values = panel[:, D:].reshape(HIST_EV, HEADS, HEAD_DIM)
        query = lax.dynamic_index_in_dim(queries, position, 1, keepdims=False).astype(jnp.float32)
        scores = jnp.einsum('chd,ehd->hce', query, keys)
        keep = (events < live[position]).astype(jnp.float32) / live[position]
        weights = (jax.nn.silu(scores * scale) * keep).astype(jnp.bfloat16)
        return jnp.einsum('hce,ehd->chd', weights.astype(jnp.float32), values)
    mixed = lax.map(one_request, slot_ids)
    attn = jnp.moveaxis(mixed, 0, 1).reshape(CANDS, REQUESTS, D)
    gated = (layer_norm(attn) * gates).astype(jnp.bfloat16).reshape(CANDS * REQUESTS, D)
    result = jnp.dot(gated, w_out, preferred_element_type=jnp.float32) + inputs.reshape(CANDS * REQUESTS, D)
    return result.astype(jnp.bfloat16).reshape(CANDS, REQUESTS, D)
```

```python
import jax
import jax.numpy as jnp
from jax import lax
from jax.sharding import PartitionSpec as P

HEADS = 8
BLK = 128


def layer_norm(values):
    center = values - jnp.mean(values, axis=-1, keepdims=True)
    spread = jnp.mean(center * center, axis=-1, keepdims=True)
    return center * lax.rsqrt(spread + 1e-05)


def routing(cache_request, rank_request, per_group):
    slot_ids = jnp.arange(cache_request.shape[0], dtype=jnp.int32)
    match = cache_request[:, None] == rank_request[None, :]
    rank_pos = jnp.sum(jnp.where(match, slot_ids[None, :], 0), axis=1)
    target = rank_pos // per_group
    owner_grp = slot_ids // per_group
    earlier = (
        (owner_grp[:, None] == owner_grp[None, :])
        & (target[:, None] == target[None, :])
        & (slot_ids[None, :] < slot_ids[:, None])
    )
    arrival = jnp.sum(earlier.astype(jnp.int32), axis=1)
    slot_of_pos = jnp.sum(jnp.where(match, slot_ids[:, None], 0), axis=0)
    return (target, arrival, slot_of_pos)


def attend_local(queries, piece, live, first_event, scale):
    rows, count = piece.shape[0], piece.shape[1]
    heads, head_dim = queries.shape[2], queries.shape[3]
    width = heads * head_dim
    keys = piece[:, :, :width].reshape(rows, count, heads, head_dim)
    values = piece[:, :, width:].reshape(rows, count, heads, head_dim)
    scores = jnp.einsum("rchd,rehd->rhce", queries, keys, preferred_element_type=jnp.float32)
    events = (first_event + jnp.arange(count)).astype(jnp.float32)
    keep = (events[None, :] < live[:, None]).astype(jnp.float32) / live[:, None]
    weights = (jax.nn.silu(scores * scale) * keep[:, None, None, :]).astype(jnp.bfloat16)
    return jnp.einsum("rhce,rehd->rchd", weights, values, preferred_element_type=jnp.float32)


def on_device(candidates, kv_cache, cache_request, rank_request, hist_blocks, w_uq, w_out):
    groups = lax.axis_size("group")
    per_group = kv_cache.shape[0]
    cand_rows = candidates.shape[0]
    width = candidates.shape[2]
    head_dim = width // HEADS
    count = kv_cache.shape[1]
    capacity = (per_group + groups - 1) // groups
    group_now = lax.axis_index("group")
    member_now = lax.axis_index("member")
    target, arrival, slot_of_pos = routing(cache_request, rank_request, per_group)
    first_slot = group_now * per_group
    local_target = lax.dynamic_slice_in_dim(target, first_slot, per_group)
    local_arrival = lax.dynamic_slice_in_dim(arrival, first_slot, per_group)
    row_index = local_target * capacity + local_arrival
    target_grid = jnp.arange(groups)[:, None, None]
    place_grid = jnp.arange(capacity)[None, :, None]
    hits = (local_target[None, None, :] == target_grid) & (
        local_arrival[None, None, :] == place_grid
    )
    chosen = jnp.sum(jnp.where(hits, jnp.arange(per_group)[None, None, :], 0), axis=2).reshape(-1)
    filled = jnp.any(hits, axis=2).reshape(-1)
    positions = first_slot + jnp.arange(per_group)
    source_slot = slot_of_pos[positions]
    receive_index = source_slot // per_group * capacity + arrival[source_slot]
    send_hits = receive_index[None, :] == jnp.arange(groups * capacity)[:, None]
    send_pos = jnp.sum(jnp.where(send_hits, jnp.arange(per_group)[None, :], 0), axis=1)
    send_filled = jnp.any(send_hits, axis=1)
    row_live = (hist_blocks[cache_request[first_slot + jnp.arange(per_group)]] * BLK).astype(
        jnp.float32
    )

    inputs = candidates.astype(jnp.float32)
    normed = layer_norm(inputs).astype(jnp.bfloat16).reshape(cand_rows * per_group, width)
    projected = jax.nn.silu(jnp.dot(normed, w_uq, preferred_element_type=jnp.float32))
    gates = projected[:, :width].reshape(cand_rows, per_group, width)
    queries = projected[:, width:].astype(jnp.bfloat16).reshape(cand_rows, per_group, width)
    scale = head_dim ** (-0.5)

    q_pos = jnp.swapaxes(queries, 0, 1)
    q_out = jnp.where(send_filled[:, None, None], q_pos[send_pos], jnp.zeros((), jnp.bfloat16))
    q_in = lax.all_to_all(q_out, "group", split_axis=0, concat_axis=0, tiled=True)
    q_rows = q_in[row_index]
    q_all = lax.all_gather(q_rows, "member", axis=1, tiled=True)
    q_all = q_all.reshape(per_group, q_all.shape[1], HEADS, head_dim)

    partial = attend_local(q_all, kv_cache, row_live, member_now * count, scale)
    partial = partial.reshape(per_group, partial.shape[1], width)
    summed = lax.psum_scatter(partial, "member", scatter_dimension=1, tiled=True)

    a_out = jnp.where(filled[:, None, None], summed[chosen], jnp.zeros((), jnp.float32))
    a_in = lax.all_to_all(a_out, "group", split_axis=0, concat_axis=0, tiled=True)
    attn = jnp.swapaxes(a_in[receive_index], 0, 1)

    gated = (layer_norm(attn) * gates).astype(jnp.bfloat16).reshape(cand_rows * per_group, width)
    result = jnp.dot(gated, w_out, preferred_element_type=jnp.float32) + inputs.reshape(
        cand_rows * per_group, width
    )
    return result.astype(jnp.bfloat16).reshape(cand_rows, per_group, width)


def solution(mesh):
    return jax.shard_map(
        on_device,
        mesh=mesh,
        in_specs=(P("member", "group", None), P("group", "member", None), P(), P(), P(), P(), P()),
        out_specs=P("member", "group", None),
        check_vma=False,
    )
```

```python
import functools

import jax
import jax.numpy as jnp
from jax import lax
from jax.experimental import pallas as pl
from jax.experimental.pallas import tpu as pltpu
from jax.sharding import PartitionSpec as P

HEADS = 8
BLK = 128


def layer_norm(values):
    center = values - jnp.mean(values, axis=-1, keepdims=True)
    spread = jnp.mean(center * center, axis=-1, keepdims=True)
    return center * lax.rsqrt(spread + 1e-05)


def routing(cache_request, rank_request, per_group):
    slot_ids = jnp.arange(cache_request.shape[0], dtype=jnp.int32)
    match = cache_request[:, None] == rank_request[None, :]
    rank_pos = jnp.sum(jnp.where(match, slot_ids[None, :], 0), axis=1)
    target = rank_pos // per_group
    owner_grp = slot_ids // per_group
    earlier = (
        (owner_grp[:, None] == owner_grp[None, :])
        & (target[:, None] == target[None, :])
        & (slot_ids[None, :] < slot_ids[:, None])
    )
    arrival = jnp.sum(earlier.astype(jnp.int32), axis=1)
    slot_of_pos = jnp.sum(jnp.where(match, slot_ids[:, None], 0), axis=0)
    return (target, arrival, slot_of_pos)


def attend_kernel(n_live_ref, q_ref, kv_ref, keep_ref, o_ref, *, heads, head_dim, scale):
    row = pl.program_id(0)
    width = heads * head_dim

    @pl.when(n_live_ref[row] <= 0)
    def _():
        o_ref[...] = jnp.zeros(o_ref.shape, o_ref.dtype)

    @pl.when(n_live_ref[row] > 0)
    def _():
        keep = keep_ref[0]
        for h in range(heads):
            lo = h * head_dim
            q = q_ref[0, :, lo:lo + head_dim]
            k = kv_ref[0, :, lo:lo + head_dim]
            v = kv_ref[0, :, width + lo:width + lo + head_dim]
            s = lax.dot_general(q, k, (((1,), (1,)), ((), ())), preferred_element_type=jnp.float32)
            w = (jax.nn.silu(s * scale) * keep).astype(jnp.bfloat16)
            o = jnp.dot(w, v, preferred_element_type=jnp.float32)
            o_ref[0, :, lo:lo + head_dim] = o.astype(o_ref.dtype)


def attend_local(queries, piece, live, first_event, scale, heads, out_dtype):
    rows, cands, width = queries.shape
    count = piece.shape[1]
    head_dim = width // heads
    events = (first_event + jnp.arange(count)).astype(jnp.float32)
    keep = ((events[None, :] < live[:, None]).astype(jnp.float32) / live[:, None])[:, None, :]
    n_live = jnp.clip(live.astype(jnp.int32) - first_event, 0, count).astype(jnp.int32)
    kernel = functools.partial(attend_kernel, heads=heads, head_dim=head_dim, scale=scale)
    flops = 4 * rows * cands * count * width
    return pl.pallas_call(
        kernel,
        out_shape=jax.ShapeDtypeStruct((rows, cands, width), out_dtype),
        grid_spec=pltpu.PrefetchScalarGridSpec(
            num_scalar_prefetch=1,
            grid=(rows,),
            in_specs=[
                pl.BlockSpec((1, cands, width), lambda r, n: (r, 0, 0)),
                pl.BlockSpec((1, count, 2 * width), lambda r, n: (r, 0, 0)),
                pl.BlockSpec((1, 1, count), lambda r, n: (r, 0, 0)),
            ],
            out_specs=pl.BlockSpec((1, cands, width), lambda r, n: (r, 0, 0)),
        ),
        cost_estimate=pl.CostEstimate(
            flops=flops,
            transcendentals=rows * cands * count * heads,
            bytes_accessed=rows * (cands * width * 4 + count * width * 4),
        ),
    )(n_live, queries, piece, keep)


def on_device(candidates, kv_cache, cache_request, rank_request, hist_blocks, w_uq, w_out):
    groups = lax.axis_size("group")
    per_group = kv_cache.shape[0]
    cand_rows = candidates.shape[0]
    width = candidates.shape[2]
    head_dim = width // HEADS
    count = kv_cache.shape[1]
    capacity = (per_group + groups - 1) // groups
    group_now = lax.axis_index("group")
    member_now = lax.axis_index("member")
    target, arrival, slot_of_pos = routing(cache_request, rank_request, per_group)
    first_slot = group_now * per_group
    local_target = lax.dynamic_slice_in_dim(target, first_slot, per_group)
    local_arrival = lax.dynamic_slice_in_dim(arrival, first_slot, per_group)
    row_index = local_target * capacity + local_arrival
    target_grid = jnp.arange(groups)[:, None, None]
    place_grid = jnp.arange(capacity)[None, :, None]
    hits = (local_target[None, None, :] == target_grid) & (
        local_arrival[None, None, :] == place_grid
    )
    chosen = jnp.sum(jnp.where(hits, jnp.arange(per_group)[None, None, :], 0), axis=2).reshape(-1)
    filled = jnp.any(hits, axis=2).reshape(-1)
    positions = first_slot + jnp.arange(per_group)
    source_slot = slot_of_pos[positions]
    receive_index = source_slot // per_group * capacity + arrival[source_slot]
    send_hits = receive_index[None, :] == jnp.arange(groups * capacity)[:, None]
    send_pos = jnp.sum(jnp.where(send_hits, jnp.arange(per_group)[None, :], 0), axis=1)
    send_filled = jnp.any(send_hits, axis=1)
    row_live = (hist_blocks[cache_request[first_slot + jnp.arange(per_group)]] * BLK).astype(
        jnp.float32
    )

    inputs = candidates.astype(jnp.float32)
    normed = layer_norm(inputs).astype(jnp.bfloat16).reshape(cand_rows * per_group, width)
    projected = jax.nn.silu(jnp.dot(normed, w_uq, preferred_element_type=jnp.float32))
    gates = projected[:, :width].reshape(cand_rows, per_group, width)
    queries = projected[:, width:].astype(jnp.bfloat16).reshape(cand_rows, per_group, width)
    scale = head_dim ** (-0.5)

    q_pos = jnp.swapaxes(queries, 0, 1)
    q_out = jnp.where(send_filled[:, None, None], q_pos[send_pos], jnp.zeros((), jnp.bfloat16))
    q_in = lax.all_to_all(q_out, "group", split_axis=0, concat_axis=0, tiled=True)
    q_rows = q_in[row_index]
    q_all = lax.all_gather(q_rows, "member", axis=1, tiled=True)

    partial = attend_local(q_all, kv_cache, row_live, member_now * count, scale, HEADS, jnp.bfloat16)
    summed = lax.psum_scatter(partial, "member", scatter_dimension=1, tiled=True)

    a_out = jnp.where(filled[:, None, None], summed[chosen], jnp.zeros((), summed.dtype))
    a_in = lax.all_to_all(a_out, "group", split_axis=0, concat_axis=0, tiled=True)
    attn = jnp.swapaxes(a_in[receive_index], 0, 1).astype(jnp.float32)

    gated = (layer_norm(attn) * gates).astype(jnp.bfloat16).reshape(cand_rows * per_group, width)
    result = jnp.dot(gated, w_out, preferred_element_type=jnp.float32) + inputs.reshape(
        cand_rows * per_group, width
    )
    return result.astype(jnp.bfloat16).reshape(cand_rows, per_group, width)


def solution(mesh):
    return jax.shard_map(
        on_device,
        mesh=mesh,
        in_specs=(P("member", "group", None), P("group", "member", None), P(), P(), P(), P(), P()),
        out_specs=P("member", "group", None),
        check_vma=False,
    )
```

```python
import functools

import jax
import jax.numpy as jnp
from jax import lax
from jax.experimental import pallas as pl
from jax.experimental.pallas import tpu as pltpu
from jax.sharding import PartitionSpec as P

HEADS = 8
BLK = 128


def layer_norm(values):
    center = values - jnp.mean(values, axis=-1, keepdims=True)
    spread = jnp.mean(center * center, axis=-1, keepdims=True)
    return center * lax.rsqrt(spread + 1e-05)


def routing(cache_request, rank_request, per_group):
    slot_ids = jnp.arange(cache_request.shape[0], dtype=jnp.int32)
    match = cache_request[:, None] == rank_request[None, :]
    rank_pos = jnp.sum(jnp.where(match, slot_ids[None, :], 0), axis=1)
    target = rank_pos // per_group
    owner_grp = slot_ids // per_group
    earlier = (
        (owner_grp[:, None] == owner_grp[None, :])
        & (target[:, None] == target[None, :])
        & (slot_ids[None, :] < slot_ids[:, None])
    )
    arrival = jnp.sum(earlier.astype(jnp.int32), axis=1)
    slot_of_pos = jnp.sum(jnp.where(match, slot_ids[:, None], 0), axis=0)
    return (target, arrival, slot_of_pos)


def attend_kernel(n_live_ref, q_ref, kv_ref, keep_ref, o_ref, *, heads, head_dim, scale):
    row = pl.program_id(0)
    width = heads * head_dim

    @pl.when(n_live_ref[row] <= 0)
    def _():
        o_ref[...] = jnp.zeros(o_ref.shape, o_ref.dtype)

    @pl.when(n_live_ref[row] > 0)
    def _():
        keep = keep_ref[0]
        for h in range(heads):
            lo = h * head_dim
            q = q_ref[0, :, lo:lo + head_dim]
            k = kv_ref[0, :, lo:lo + head_dim]
            v = kv_ref[0, :, width + lo:width + lo + head_dim]
            s = lax.dot_general(q, k, (((1,), (1,)), ((), ())), preferred_element_type=jnp.float32)
            w = (jax.nn.silu(s * scale) * keep).astype(jnp.bfloat16)
            o = jnp.dot(w, v, preferred_element_type=jnp.float32)
            o_ref[0, :, lo:lo + head_dim] = o.astype(o_ref.dtype)


def attend_local(queries, piece, live, first_event, scale, heads, out_dtype):
    rows, cands, width = queries.shape
    count = piece.shape[1]
    head_dim = width // heads
    events = (first_event + jnp.arange(count)).astype(jnp.float32)
    keep = ((events[None, :] < live[:, None]).astype(jnp.float32) / live[:, None])[:, None, :]
    n_live = jnp.clip(live.astype(jnp.int32) - first_event, 0, count).astype(jnp.int32)
    kernel = functools.partial(attend_kernel, heads=heads, head_dim=head_dim, scale=scale)
    flops = 4 * rows * cands * count * width
    return pl.pallas_call(
        kernel,
        out_shape=jax.ShapeDtypeStruct((rows, cands, width), out_dtype),
        grid_spec=pltpu.PrefetchScalarGridSpec(
            num_scalar_prefetch=1,
            grid=(rows,),
            in_specs=[
                pl.BlockSpec((1, cands, width), lambda r, n: (r, 0, 0)),
                pl.BlockSpec((1, count, 2 * width), lambda r, n: (r, 0, 0)),
                pl.BlockSpec((1, 1, count), lambda r, n: (r, 0, 0)),
            ],
            out_specs=pl.BlockSpec((1, cands, width), lambda r, n: (r, 0, 0)),
        ),
        cost_estimate=pl.CostEstimate(
            flops=flops,
            transcendentals=rows * cands * count * heads,
            bytes_accessed=rows * (cands * width * 4 + count * width * 4),
        ),
    )(n_live, queries, piece, keep)


def shift_perm(grid, axis, shift):
    rows, cols = grid
    pairs = []
    for zi in range(rows):
        for xi in range(cols):
            if axis == 0:
                dst = ((zi + shift) % rows) * cols + xi
            else:
                dst = zi * cols + (xi + shift) % cols
            pairs.append((zi * cols + xi, dst))
    return pairs


def send(value, grid, axis, shift):
    return lax.ppermute(value, "member", shift_perm(grid, axis, shift))


def ring_gather(block, grid, axis):
    n = grid[axis]
    slots = {0: block}
    ahead, behind = block, block
    for k in range(1, (n - 1) // 2 + 1):
        ahead = send(ahead, grid, axis, -1)
        behind = send(behind, grid, axis, 1)
        slots[k], slots[n - k] = ahead, behind
    if n % 2 == 0:
        if n == 2:
            slots[1] = send(block, grid, axis, -1)
        else:
            half = block.shape[1] // 2
            first = send(behind[:, :half], grid, axis, 1)
            second = send(ahead[:, half:], grid, axis, -1)
            slots[n // 2] = jnp.concatenate([first, second], axis=1)
    return jnp.concatenate([slots[r] for r in range(n)], axis=1)


def ring_reduce(parts, grid, axis):
    n = grid[axis]
    rows, total, width = parts.shape
    m = total // n
    slots = [parts[:, r * m:(r + 1) * m].astype(jnp.float32) for r in range(n)]
    if n == 1:
        return slots[0]
    if n == 2:
        return slots[0] + send(slots[1].astype(jnp.bfloat16), grid, axis, 1).astype(jnp.float32)
    top = (n - 1) // 2
    acc_ahead, acc_behind = slots[top], slots[n - top]
    if n % 2 == 0:
        half = m // 2
        far = slots[n // 2].astype(jnp.bfloat16)
        got_first = send(far[:, :half], grid, axis, 1).astype(jnp.float32)
        got_second = send(far[:, half:], grid, axis, -1).astype(jnp.float32)
        acc_ahead = acc_ahead + jnp.concatenate([got_first, jnp.zeros_like(got_first)], axis=1)
        acc_behind = acc_behind + jnp.concatenate([jnp.zeros_like(got_second), got_second], axis=1)
    for k in range(top, 0, -1):
        got_ahead = send(acc_ahead.astype(jnp.bfloat16), grid, axis, 1).astype(jnp.float32)
        got_behind = send(acc_behind.astype(jnp.bfloat16), grid, axis, -1).astype(jnp.float32)
        if k > 1:
            acc_ahead = slots[k - 1] + got_ahead
            acc_behind = slots[n - k + 1] + got_behind
        else:
            return slots[0] + got_ahead + got_behind


def torus_gather(block, grid, order):
    rows, m, width = block.shape
    out = ring_gather(block, grid, order[1])
    return ring_gather(out, grid, order[0])


def torus_reduce(parts, grid, order):
    out = ring_reduce(parts, grid, order[0])
    return ring_reduce(out, grid, order[1])


def on_device(grid, candidates, kv_cache, cache_request, rank_request, hist_blocks, w_uq, w_out):
    groups = lax.axis_size("group")
    per_group = kv_cache.shape[0]
    cand_rows = candidates.shape[0]
    width = candidates.shape[2]
    head_dim = width // HEADS
    count = kv_cache.shape[1]
    capacity = (per_group + groups - 1) // groups
    group_now = lax.axis_index("group")
    member_now = lax.axis_index("member")
    target, arrival, slot_of_pos = routing(cache_request, rank_request, per_group)
    first_slot = group_now * per_group
    local_target = lax.dynamic_slice_in_dim(target, first_slot, per_group)
    local_arrival = lax.dynamic_slice_in_dim(arrival, first_slot, per_group)
    row_index = local_target * capacity + local_arrival
    target_grid = jnp.arange(groups)[:, None, None]
    place_grid = jnp.arange(capacity)[None, :, None]
    hits = (local_target[None, None, :] == target_grid) & (
        local_arrival[None, None, :] == place_grid
    )
    chosen = jnp.sum(jnp.where(hits, jnp.arange(per_group)[None, None, :], 0), axis=2).reshape(-1)
    filled = jnp.any(hits, axis=2).reshape(-1)
    positions = first_slot + jnp.arange(per_group)
    source_slot = slot_of_pos[positions]
    receive_index = source_slot // per_group * capacity + arrival[source_slot]
    send_hits = receive_index[None, :] == jnp.arange(groups * capacity)[:, None]
    send_pos = jnp.sum(jnp.where(send_hits, jnp.arange(per_group)[None, :], 0), axis=1)
    send_filled = jnp.any(send_hits, axis=1)
    row_live = (hist_blocks[cache_request[first_slot + jnp.arange(per_group)]] * BLK).astype(
        jnp.float32
    )

    inputs = candidates.astype(jnp.float32)
    normed = layer_norm(inputs).astype(jnp.bfloat16).reshape(cand_rows * per_group, width)
    projected = jax.nn.silu(jnp.dot(normed, w_uq, preferred_element_type=jnp.float32))
    gates = projected[:, :width].reshape(cand_rows, per_group, width)
    queries = projected[:, width:].astype(jnp.bfloat16).reshape(cand_rows, per_group, width)
    scale = head_dim ** (-0.5)

    q_pos = jnp.swapaxes(queries, 0, 1)
    q_out = jnp.where(send_filled[:, None, None], q_pos[send_pos], jnp.zeros((), jnp.bfloat16))
    q_in = lax.all_to_all(q_out, "group", split_axis=0, concat_axis=0, tiled=True)
    q_rows = q_in[row_index]
    split = per_group // 2
    halves = ((slice(0, split), (0, 1)), (slice(split, per_group), (1, 0)))
    sums = []
    for rows_of, order in halves:
        q_all = torus_gather(q_rows[rows_of], grid, order)
        partial = attend_local(
            q_all, kv_cache[rows_of], row_live[rows_of], member_now * count, scale, HEADS, jnp.bfloat16
        )
        sums.append(torus_reduce(partial, grid, order))
    summed = jnp.concatenate(sums, axis=0).astype(jnp.bfloat16)

    a_out = jnp.where(filled[:, None, None], summed[chosen], jnp.zeros((), summed.dtype))
    a_in = lax.all_to_all(a_out, "group", split_axis=0, concat_axis=0, tiled=True)
    attn = jnp.swapaxes(a_in[receive_index], 0, 1).astype(jnp.float32)

    gated = (layer_norm(attn) * gates).astype(jnp.bfloat16).reshape(cand_rows * per_group, width)
    result = jnp.dot(gated, w_out, preferred_element_type=jnp.float32) + inputs.reshape(
        cand_rows * per_group, width
    )
    return result.astype(jnp.bfloat16).reshape(cand_rows, per_group, width)


def member_grid(mesh):
    members = mesh.shape["member"]
    try:
        line = mesh.devices[0]
        cols = len({d.coords[0] for d in line})
    except (AttributeError, TypeError, IndexError):
        cols = int(round(members ** 0.5))
    if cols < 1 or members % cols:
        cols = members
    return (members // cols, cols)


def solution(mesh):
    return jax.shard_map(
        functools.partial(on_device, member_grid(mesh)),
        mesh=mesh,
        in_specs=(P("member", "group", None), P("group", "member", None), P(), P(), P(), P(), P()),
        out_specs=P("member", "group", None),
        check_vma=False,
    )
```

```python
import functools

import jax
import jax.numpy as jnp
from jax import lax
from jax.experimental import pallas as pl
from jax.experimental.pallas import tpu as pltpu
from jax.sharding import PartitionSpec as P

HEADS = 8
BLK = 128


def layer_norm(values):
    center = values - jnp.mean(values, axis=-1, keepdims=True)
    spread = jnp.mean(center * center, axis=-1, keepdims=True)
    return center * lax.rsqrt(spread + 1e-05)


def routing(cache_request, rank_request, per_group):
    slot_ids = jnp.arange(cache_request.shape[0], dtype=jnp.int32)
    match = cache_request[:, None] == rank_request[None, :]
    rank_pos = jnp.sum(jnp.where(match, slot_ids[None, :], 0), axis=1)
    target = rank_pos // per_group
    owner_grp = slot_ids // per_group
    earlier = (
        (owner_grp[:, None] == owner_grp[None, :])
        & (target[:, None] == target[None, :])
        & (slot_ids[None, :] < slot_ids[:, None])
    )
    arrival = jnp.sum(earlier.astype(jnp.int32), axis=1)
    slot_of_pos = jnp.sum(jnp.where(match, slot_ids[:, None], 0), axis=0)
    return (target, arrival, slot_of_pos)


def attend_kernel(n_live_ref, q_ref, kv_ref, keep_ref, o_ref, *, heads, head_dim, scale):
    row = pl.program_id(0)
    width = heads * head_dim

    @pl.when(n_live_ref[row] <= 0)
    def _():
        o_ref[...] = jnp.zeros(o_ref.shape, o_ref.dtype)

    @pl.when(n_live_ref[row] > 0)
    def _():
        keep = keep_ref[0]
        for h in range(heads):
            lo = h * head_dim
            q = q_ref[0, :, lo:lo + head_dim]
            k = kv_ref[0, :, lo:lo + head_dim]
            v = kv_ref[0, :, width + lo:width + lo + head_dim]
            s = lax.dot_general(q, k, (((1,), (1,)), ((), ())), preferred_element_type=jnp.float32)
            w = (jax.nn.silu(s * scale) * keep).astype(jnp.bfloat16)
            o = jnp.dot(w, v, preferred_element_type=jnp.float32)
            o_ref[0, :, lo:lo + head_dim] = o.astype(o_ref.dtype)


def attend_local(queries, piece, live, first_event, scale, heads, out_dtype):
    rows, cands, width = queries.shape
    count = piece.shape[1]
    head_dim = width // heads
    events = (first_event + jnp.arange(count)).astype(jnp.float32)
    keep = ((events[None, :] < live[:, None]).astype(jnp.float32) / live[:, None])[:, None, :]
    n_live = jnp.clip(live.astype(jnp.int32) - first_event, 0, count).astype(jnp.int32)
    kernel = functools.partial(attend_kernel, heads=heads, head_dim=head_dim, scale=scale)
    flops = 4 * rows * cands * count * width
    return pl.pallas_call(
        kernel,
        out_shape=jax.ShapeDtypeStruct((rows, cands, width), out_dtype),
        grid_spec=pltpu.PrefetchScalarGridSpec(
            num_scalar_prefetch=1,
            grid=(rows,),
            in_specs=[
                pl.BlockSpec((1, cands, width), lambda r, n: (r, 0, 0)),
                pl.BlockSpec((1, count, 2 * width), lambda r, n: (r, 0, 0)),
                pl.BlockSpec((1, 1, count), lambda r, n: (r, 0, 0)),
            ],
            out_specs=pl.BlockSpec((1, cands, width), lambda r, n: (r, 0, 0)),
        ),
        cost_estimate=pl.CostEstimate(
            flops=flops,
            transcendentals=rows * cands * count * heads,
            bytes_accessed=rows * (cands * width * 4 + count * width * 4),
        ),
    )(n_live, queries, piece, keep)


def shift_perm(grid, axis, shift):
    rows, cols = grid
    pairs = []
    for zi in range(rows):
        for xi in range(cols):
            if axis == 0:
                dst = ((zi + shift) % rows) * cols + xi
            else:
                dst = zi * cols + (xi + shift) % cols
            pairs.append((zi * cols + xi, dst))
    return pairs


def send(value, grid, axis, shift):
    return lax.ppermute(value, "member", shift_perm(grid, axis, shift))


def ring_gather_slots(block, grid, axis):
    n = grid[axis]
    slots = {0: block}
    ahead, behind = block, block
    for k in range(1, (n - 1) // 2 + 1):
        ahead = send(ahead, grid, axis, -1)
        behind = send(behind, grid, axis, 1)
        slots[k], slots[n - k] = ahead, behind
    if n % 2 == 0:
        if n == 2:
            slots[1] = send(block, grid, axis, -1)
        else:
            half = block.shape[1] // 2
            first = send(behind[:, :half], grid, axis, 1)
            second = send(ahead[:, half:], grid, axis, -1)
            slots[n // 2] = jnp.concatenate([first, second], axis=1)
    return [slots[r] for r in range(n)]


def ring_gather(block, grid, axis):
    return jnp.concatenate(ring_gather_slots(block, grid, axis), axis=1)


def ring_reduce_slots(parts, grid, axis):
    n = grid[axis]
    m = parts[0].shape[1]
    slots = [p.astype(jnp.float32) for p in parts]
    if n == 1:
        return slots[0]
    if n == 2:
        return slots[0] + send(parts[1].astype(jnp.bfloat16), grid, axis, 1).astype(jnp.float32)
    top = (n - 1) // 2
    acc_ahead, acc_behind = slots[top], slots[n - top]
    if n % 2 == 0:
        half = m // 2
        far = parts[n // 2].astype(jnp.bfloat16)
        got_first = send(far[:, :half], grid, axis, 1).astype(jnp.float32)
        got_second = send(far[:, half:], grid, axis, -1).astype(jnp.float32)
        acc_ahead = acc_ahead + jnp.concatenate([got_first, jnp.zeros_like(got_first)], axis=1)
        acc_behind = acc_behind + jnp.concatenate([jnp.zeros_like(got_second), got_second], axis=1)
    for k in range(top, 0, -1):
        got_ahead = send(acc_ahead.astype(jnp.bfloat16), grid, axis, 1).astype(jnp.float32)
        got_behind = send(acc_behind.astype(jnp.bfloat16), grid, axis, -1).astype(jnp.float32)
        if k > 1:
            acc_ahead = slots[k - 1] + got_ahead
            acc_behind = slots[n - k + 1] + got_behind
        else:
            return slots[0] + got_ahead + got_behind


def ring_reduce(parts, grid, axis):
    n = grid[axis]
    m = parts.shape[1] // n
    return ring_reduce_slots([parts[:, r * m:(r + 1) * m] for r in range(n)], grid, axis)


def torus_gather(block, grid, order):
    rows, m, width = block.shape
    out = ring_gather(block, grid, order[1])
    return ring_gather(out, grid, order[0])


def torus_reduce(parts, grid, order):
    out = ring_reduce(parts, grid, order[0])
    return ring_reduce(out, grid, order[1])


def on_device(grid, candidates, kv_cache, cache_request, rank_request, hist_blocks, w_uq, w_out):
    groups = lax.axis_size("group")
    per_group = kv_cache.shape[0]
    cand_rows = candidates.shape[0]
    width = candidates.shape[2]
    head_dim = width // HEADS
    count = kv_cache.shape[1]
    capacity = (per_group + groups - 1) // groups
    group_now = lax.axis_index("group")
    member_now = lax.axis_index("member")
    target, arrival, slot_of_pos = routing(cache_request, rank_request, per_group)
    first_slot = group_now * per_group
    local_target = lax.dynamic_slice_in_dim(target, first_slot, per_group)
    local_arrival = lax.dynamic_slice_in_dim(arrival, first_slot, per_group)
    row_index = local_target * capacity + local_arrival
    target_grid = jnp.arange(groups)[:, None, None]
    place_grid = jnp.arange(capacity)[None, :, None]
    hits = (local_target[None, None, :] == target_grid) & (
        local_arrival[None, None, :] == place_grid
    )
    chosen = jnp.sum(jnp.where(hits, jnp.arange(per_group)[None, None, :], 0), axis=2).reshape(-1)
    filled = jnp.any(hits, axis=2).reshape(-1)
    positions = first_slot + jnp.arange(per_group)
    source_slot = slot_of_pos[positions]
    receive_index = source_slot // per_group * capacity + arrival[source_slot]
    send_hits = receive_index[None, :] == jnp.arange(groups * capacity)[:, None]
    send_pos = jnp.sum(jnp.where(send_hits, jnp.arange(per_group)[None, :], 0), axis=1)
    send_filled = jnp.any(send_hits, axis=1)
    row_live = (hist_blocks[cache_request[first_slot + jnp.arange(per_group)]] * BLK).astype(
        jnp.float32
    )

    inputs = candidates.astype(jnp.float32)
    normed = layer_norm(inputs).astype(jnp.bfloat16).reshape(cand_rows * per_group, width)
    projected = jax.nn.silu(jnp.dot(normed, w_uq, preferred_element_type=jnp.float32))
    gates = projected[:, :width].reshape(cand_rows, per_group, width)
    queries = projected[:, width:].astype(jnp.bfloat16).reshape(cand_rows, per_group, width)
    scale = head_dim ** (-0.5)

    q_pos = jnp.swapaxes(queries, 0, 1)
    q_out = jnp.where(send_filled[:, None, None], q_pos[send_pos], jnp.zeros((), jnp.bfloat16))
    q_in = lax.all_to_all(q_out, "group", split_axis=0, concat_axis=0, tiled=True)
    q_rows = q_in[row_index]
    split = per_group // 2
    halves = ((slice(0, split), (0, 1)), (slice(split, per_group), (1, 0)))
    sums = []
    for rows_of, order in halves:
        inner = ring_gather(q_rows[rows_of], grid, order[1])
        partials = [
            attend_local(
                q_slot, kv_cache[rows_of], row_live[rows_of], member_now * count, scale, HEADS, jnp.bfloat16
            )
            for q_slot in ring_gather_slots(inner, grid, order[0])
        ]
        outer = ring_reduce_slots(partials, grid, order[0]).astype(jnp.bfloat16)
        sums.append(ring_reduce(outer, grid, order[1]))
    summed = jnp.concatenate(sums, axis=0).astype(jnp.bfloat16)

    a_out = jnp.where(filled[:, None, None], summed[chosen], jnp.zeros((), summed.dtype))
    a_in = lax.all_to_all(a_out, "group", split_axis=0, concat_axis=0, tiled=True)
    attn = jnp.swapaxes(a_in[receive_index], 0, 1).astype(jnp.float32)

    gated = (layer_norm(attn) * gates).astype(jnp.bfloat16).reshape(cand_rows * per_group, width)
    result = jnp.dot(gated, w_out, preferred_element_type=jnp.float32) + inputs.reshape(
        cand_rows * per_group, width
    )
    return result.astype(jnp.bfloat16).reshape(cand_rows, per_group, width)


def member_grid(mesh):
    members = mesh.shape["member"]
    try:
        line = mesh.devices[0]
        cols = len({d.coords[0] for d in line})
    except (AttributeError, TypeError, IndexError):
        cols = int(round(members ** 0.5))
    if cols < 1 or members % cols:
        cols = members
    return (members // cols, cols)


def solution(mesh):
    return jax.shard_map(
        functools.partial(on_device, member_grid(mesh)),
        mesh=mesh,
        in_specs=(P("member", "group", None), P("group", "member", None), P(), P(), P(), P(), P()),
        out_specs=P("member", "group", None),
        check_vma=False,
    )
```

```python
import functools

import jax
import jax.numpy as jnp
from jax import lax
from jax.experimental import pallas as pl
from jax.experimental.pallas import tpu as pltpu
from jax.sharding import PartitionSpec as P

HEADS = 8
BLK = 128


def layer_norm(values):
    center = values - jnp.mean(values, axis=-1, keepdims=True)
    spread = jnp.mean(center * center, axis=-1, keepdims=True)
    return center * lax.rsqrt(spread + 1e-05)


def routing(cache_request, rank_request, per_group):
    slot_ids = jnp.arange(cache_request.shape[0], dtype=jnp.int32)
    match = cache_request[:, None] == rank_request[None, :]
    rank_pos = jnp.sum(jnp.where(match, slot_ids[None, :], 0), axis=1)
    target = rank_pos // per_group
    owner_grp = slot_ids // per_group
    earlier = (
        (owner_grp[:, None] == owner_grp[None, :])
        & (target[:, None] == target[None, :])
        & (slot_ids[None, :] < slot_ids[:, None])
    )
    arrival = jnp.sum(earlier.astype(jnp.int32), axis=1)
    slot_of_pos = jnp.sum(jnp.where(match, slot_ids[:, None], 0), axis=0)
    return (target, arrival, slot_of_pos)


def attend_kernel(n_live_ref, q_ref, kv_ref, keep_ref, o_ref, *, heads, head_dim, scale):
    row = pl.program_id(0)
    width = heads * head_dim

    @pl.when(n_live_ref[row] <= 0)
    def _():
        o_ref[...] = jnp.zeros(o_ref.shape, o_ref.dtype)

    @pl.when(n_live_ref[row] > 0)
    def _():
        keep = keep_ref[0]
        for h in range(heads):
            lo = h * head_dim
            q = q_ref[0, :, lo:lo + head_dim]
            k = kv_ref[0, :, lo:lo + head_dim]
            v = kv_ref[0, :, width + lo:width + lo + head_dim]
            s = lax.dot_general(q, k, (((1,), (1,)), ((), ())), preferred_element_type=jnp.float32)
            w = (jax.nn.silu(s * scale) * keep).astype(jnp.bfloat16)
            o = jnp.dot(w, v, preferred_element_type=jnp.float32)
            o_ref[0, :, lo:lo + head_dim] = o.astype(o_ref.dtype)


def attend_local(queries, piece, live, first_event, scale, heads, out_dtype):
    rows, cands, width = queries.shape
    count = piece.shape[1]
    head_dim = width // heads
    events = (first_event + jnp.arange(count)).astype(jnp.float32)
    keep = ((events[None, :] < live[:, None]).astype(jnp.float32) / live[:, None])[:, None, :]
    n_live = jnp.clip(live.astype(jnp.int32) - first_event, 0, count).astype(jnp.int32)
    kernel = functools.partial(attend_kernel, heads=heads, head_dim=head_dim, scale=scale)
    flops = 4 * rows * cands * count * width
    return pl.pallas_call(
        kernel,
        out_shape=jax.ShapeDtypeStruct((rows, cands, width), out_dtype),
        grid_spec=pltpu.PrefetchScalarGridSpec(
            num_scalar_prefetch=1,
            grid=(rows,),
            in_specs=[
                pl.BlockSpec((1, cands, width), lambda r, n: (r, 0, 0)),
                pl.BlockSpec((1, count, 2 * width), lambda r, n: (r, 0, 0)),
                pl.BlockSpec((1, 1, count), lambda r, n: (r, 0, 0)),
            ],
            out_specs=pl.BlockSpec((1, cands, width), lambda r, n: (r, 0, 0)),
        ),
        cost_estimate=pl.CostEstimate(
            flops=flops,
            transcendentals=rows * cands * count * heads,
            bytes_accessed=rows * (cands * width * 4 + count * width * 4),
        ),
    )(n_live, queries, piece, keep)


def shift_perm(grid, axis, shift):
    rows, cols = grid
    pairs = []
    for zi in range(rows):
        for xi in range(cols):
            if axis == 0:
                dst = ((zi + shift) % rows) * cols + xi
            else:
                dst = zi * cols + (xi + shift) % cols
            pairs.append((zi * cols + xi, dst))
    return pairs


def send(value, grid, axis, shift):
    return lax.ppermute(value, "member", shift_perm(grid, axis, shift))


def ring_gather(block, grid, axis):
    n = grid[axis]
    slots = {0: block}
    ahead, behind = block, block
    for k in range(1, (n - 1) // 2 + 1):
        ahead = send(ahead, grid, axis, -1)
        behind = send(behind, grid, axis, 1)
        slots[k], slots[n - k] = ahead, behind
    if n % 2 == 0:
        if n == 2:
            slots[1] = send(block, grid, axis, -1)
        else:
            half = block.shape[1] // 2
            first = send(behind[:, :half], grid, axis, 1)
            second = send(ahead[:, half:], grid, axis, -1)
            slots[n // 2] = jnp.concatenate([first, second], axis=1)
    return jnp.concatenate([slots[r] for r in range(n)], axis=1)


def ring_reduce_slots(parts, grid, axis):
    n = grid[axis]
    m = parts[0].shape[1]
    slots = [p.astype(jnp.float32) for p in parts]
    if n == 1:
        return slots[0]
    if n == 2:
        return slots[0] + send(parts[1].astype(jnp.bfloat16), grid, axis, 1).astype(jnp.float32)
    top = (n - 1) // 2
    acc_ahead, acc_behind = slots[top], slots[n - top]
    if n % 2 == 0:
        half = m // 2
        far = parts[n // 2].astype(jnp.bfloat16)
        got_first = send(far[:, :half], grid, axis, 1).astype(jnp.float32)
        got_second = send(far[:, half:], grid, axis, -1).astype(jnp.float32)
        acc_ahead = acc_ahead + jnp.concatenate([got_first, jnp.zeros_like(got_first)], axis=1)
        acc_behind = acc_behind + jnp.concatenate([jnp.zeros_like(got_second), got_second], axis=1)
    for k in range(top, 0, -1):
        got_ahead = send(acc_ahead.astype(jnp.bfloat16), grid, axis, 1).astype(jnp.float32)
        got_behind = send(acc_behind.astype(jnp.bfloat16), grid, axis, -1).astype(jnp.float32)
        if k > 1:
            acc_ahead = slots[k - 1] + got_ahead
            acc_behind = slots[n - k + 1] + got_behind
        else:
            return slots[0] + got_ahead + got_behind


def ring_reduce(parts, grid, axis):
    n = grid[axis]
    m = parts.shape[1] // n
    return ring_reduce_slots([parts[:, r * m:(r + 1) * m] for r in range(n)], grid, axis)


def torus_reduce_abs(parts, grid, coords, order):
    rr, total, width = parts.shape
    m = total // (grid[0] * grid[1])
    grid_parts = parts.reshape(rr, grid[0], grid[1], m, width)
    first, second = order
    n = grid[first]
    slots = [
        lax.dynamic_index_in_dim(grid_parts, (coords[first] + r) % n, 1 + first, keepdims=False).reshape(
            rr, -1, width
        )
        for r in range(n)
    ]
    out = ring_reduce_slots(slots, grid, first).astype(jnp.bfloat16)
    n = grid[second]
    out = out.reshape(rr, n, m, width)
    slots = [lax.dynamic_index_in_dim(out, (coords[second] + r) % n, 1, keepdims=False) for r in range(n)]
    return ring_reduce_slots(slots, grid, second)


def torus_gather(block, grid, order):
    rows, m, width = block.shape
    out = ring_gather(block, grid, order[1])
    return ring_gather(out, grid, order[0])


def torus_reduce(parts, grid, order):
    out = ring_reduce(parts, grid, order[0])
    return ring_reduce(out, grid, order[1])


def on_device(grid, candidates, kv_cache, cache_request, rank_request, hist_blocks, w_uq, w_out):
    groups = lax.axis_size("group")
    per_group = kv_cache.shape[0]
    cand_rows = candidates.shape[0]
    width = candidates.shape[2]
    head_dim = width // HEADS
    count = kv_cache.shape[1]
    capacity = (per_group + groups - 1) // groups
    group_now = lax.axis_index("group")
    member_now = lax.axis_index("member")
    target, arrival, slot_of_pos = routing(cache_request, rank_request, per_group)
    first_slot = group_now * per_group
    local_target = lax.dynamic_slice_in_dim(target, first_slot, per_group)
    local_arrival = lax.dynamic_slice_in_dim(arrival, first_slot, per_group)
    row_index = local_target * capacity + local_arrival
    target_grid = jnp.arange(groups)[:, None, None]
    place_grid = jnp.arange(capacity)[None, :, None]
    hits = (local_target[None, None, :] == target_grid) & (
        local_arrival[None, None, :] == place_grid
    )
    chosen = jnp.sum(jnp.where(hits, jnp.arange(per_group)[None, None, :], 0), axis=2).reshape(-1)
    filled = jnp.any(hits, axis=2).reshape(-1)
    positions = first_slot + jnp.arange(per_group)
    source_slot = slot_of_pos[positions]
    receive_index = source_slot // per_group * capacity + arrival[source_slot]
    send_hits = receive_index[None, :] == jnp.arange(groups * capacity)[:, None]
    send_pos = jnp.sum(jnp.where(send_hits, jnp.arange(per_group)[None, :], 0), axis=1)
    send_filled = jnp.any(send_hits, axis=1)
    row_live = (hist_blocks[cache_request[first_slot + jnp.arange(per_group)]] * BLK).astype(
        jnp.float32
    )

    inputs = candidates.astype(jnp.float32)
    normed = layer_norm(inputs).astype(jnp.bfloat16).reshape(cand_rows * per_group, width)
    projected = jax.nn.silu(jnp.dot(normed, w_uq, preferred_element_type=jnp.float32))
    gates = projected[:, :width].reshape(cand_rows, per_group, width)
    queries = projected[:, width:].astype(jnp.bfloat16).reshape(cand_rows, per_group, width)
    scale = head_dim ** (-0.5)

    q_pos = jnp.swapaxes(queries, 0, 1)
    q_out = jnp.where(send_filled[:, None, None], q_pos[send_pos], jnp.zeros((), jnp.bfloat16))
    q_in = lax.all_to_all(q_out, "group", split_axis=0, concat_axis=0, tiled=True)
    q_rows = q_in[row_index]
    coords = (member_now // grid[1], member_now % grid[1])
    split = per_group // 2
    halves = ((slice(0, split), (0, 1)), (slice(split, per_group), (1, 0)))
    sums = []
    for rows_of, order in halves:
        q_all = lax.all_gather(q_rows[rows_of], "member", axis=1, tiled=True)
        partial = attend_local(
            q_all, kv_cache[rows_of], row_live[rows_of], member_now * count, scale, HEADS, jnp.bfloat16
        )
        sums.append(torus_reduce_abs(partial, grid, coords, order))
    summed = jnp.concatenate(sums, axis=0).astype(jnp.bfloat16)

    a_out = jnp.where(filled[:, None, None], summed[chosen], jnp.zeros((), summed.dtype))
    a_in = lax.all_to_all(a_out, "group", split_axis=0, concat_axis=0, tiled=True)
    attn = jnp.swapaxes(a_in[receive_index], 0, 1).astype(jnp.float32)

    gated = (layer_norm(attn) * gates).astype(jnp.bfloat16).reshape(cand_rows * per_group, width)
    result = jnp.dot(gated, w_out, preferred_element_type=jnp.float32) + inputs.reshape(
        cand_rows * per_group, width
    )
    return result.astype(jnp.bfloat16).reshape(cand_rows, per_group, width)


def member_grid(mesh):
    members = mesh.shape["member"]
    try:
        line = mesh.devices[0]
        cols = len({d.coords[0] for d in line})
    except (AttributeError, TypeError, IndexError):
        cols = int(round(members ** 0.5))
    if cols < 1 or members % cols:
        cols = members
    return (members // cols, cols)


def solution(mesh):
    return jax.shard_map(
        functools.partial(on_device, member_grid(mesh)),
        mesh=mesh,
        in_specs=(P("member", "group", None), P("group", "member", None), P(), P(), P(), P(), P()),
        out_specs=P("member", "group", None),
        check_vma=False,
    )
```

```python
import functools

import jax
import jax.numpy as jnp
from jax import lax
from jax.experimental import pallas as pl
from jax.experimental.pallas import tpu as pltpu
from jax.sharding import PartitionSpec as P

HEADS = 8
BLK = 128


def layer_norm(values):
    center = values - jnp.mean(values, axis=-1, keepdims=True)
    spread = jnp.mean(center * center, axis=-1, keepdims=True)
    return center * lax.rsqrt(spread + 1e-05)


def routing(cache_request, rank_request, per_group):
    slot_ids = jnp.arange(cache_request.shape[0], dtype=jnp.int32)
    match = cache_request[:, None] == rank_request[None, :]
    rank_pos = jnp.sum(jnp.where(match, slot_ids[None, :], 0), axis=1)
    target = rank_pos // per_group
    owner_grp = slot_ids // per_group
    earlier = (
        (owner_grp[:, None] == owner_grp[None, :])
        & (target[:, None] == target[None, :])
        & (slot_ids[None, :] < slot_ids[:, None])
    )
    arrival = jnp.sum(earlier.astype(jnp.int32), axis=1)
    slot_of_pos = jnp.sum(jnp.where(match, slot_ids[:, None], 0), axis=0)
    return (target, arrival, slot_of_pos)


def attend_kernel(n_live_ref, *refs, pieces, heads, head_dim, scale):
    q_refs = refs[:pieces]
    kv_ref, keep_ref = refs[pieces], refs[pieces + 1]
    o_refs = refs[pieces + 2:]
    row = pl.program_id(0)
    width = heads * head_dim

    @pl.when(n_live_ref[row] <= 0)
    def _():
        for o_ref in o_refs:
            o_ref[...] = jnp.zeros(o_ref.shape, o_ref.dtype)

    @pl.when(n_live_ref[row] > 0)
    def _():
        keep = keep_ref[0]
        for h in range(heads):
            lo = h * head_dim
            k = kv_ref[0, :, lo:lo + head_dim]
            v = kv_ref[0, :, width + lo:width + lo + head_dim]
            for q_ref, o_ref in zip(q_refs, o_refs):
                q = q_ref[0, :, lo:lo + head_dim]
                s = lax.dot_general(q, k, (((1,), (1,)), ((), ())), preferred_element_type=jnp.float32)
                w = (jax.nn.silu(s * scale) * keep).astype(jnp.bfloat16)
                o = jnp.dot(w, v, preferred_element_type=jnp.float32)
                o_ref[0, :, lo:lo + head_dim] = o.astype(o_ref.dtype)


def attend_local(q_pieces, piece, live, first_event, scale, heads, out_dtype):
    rows, _, width = q_pieces[0].shape
    count = piece.shape[1]
    head_dim = width // heads
    cands = sum(q.shape[1] for q in q_pieces)
    events = (first_event + jnp.arange(count)).astype(jnp.float32)
    keep = ((events[None, :] < live[:, None]).astype(jnp.float32) / live[:, None])[:, None, :]
    n_live = jnp.clip(live.astype(jnp.int32) - first_event, 0, count).astype(jnp.int32)
    kernel = functools.partial(
        attend_kernel, pieces=len(q_pieces), heads=heads, head_dim=head_dim, scale=scale
    )
    flops = 4 * rows * cands * count * width
    q_specs = [pl.BlockSpec((1, q.shape[1], width), lambda r, n: (r, 0, 0)) for q in q_pieces]
    return pl.pallas_call(
        kernel,
        out_shape=[jax.ShapeDtypeStruct(q.shape, out_dtype) for q in q_pieces],
        grid_spec=pltpu.PrefetchScalarGridSpec(
            num_scalar_prefetch=1,
            grid=(rows,),
            in_specs=q_specs
            + [
                pl.BlockSpec((1, count, 2 * width), lambda r, n: (r, 0, 0)),
                pl.BlockSpec((1, 1, count), lambda r, n: (r, 0, 0)),
            ],
            out_specs=[pl.BlockSpec((1, q.shape[1], width), lambda r, n: (r, 0, 0)) for q in q_pieces],
        ),
        cost_estimate=pl.CostEstimate(
            flops=flops,
            transcendentals=rows * cands * count * heads,
            bytes_accessed=rows * (cands * width * 4 + count * width * 4),
        ),
    )(n_live, *q_pieces, piece, keep)


def shift_perm(grid, axis, shift):
    rows, cols = grid
    pairs = []
    for zi in range(rows):
        for xi in range(cols):
            if axis == 0:
                dst = ((zi + shift) % rows) * cols + xi
            else:
                dst = zi * cols + (xi + shift) % cols
            pairs.append((zi * cols + xi, dst))
    return pairs


def send(value, grid, axis, shift):
    return lax.ppermute(value, "member", shift_perm(grid, axis, shift))


def ring_gather_pieces(block, grid, axis):
    n = grid[axis]
    if n % 2 or n < 4:
        return ring_gather_slots(block, grid, axis)
    slots = {0: block}
    ahead, behind = block, block
    for k in range(1, (n - 1) // 2 + 1):
        ahead = send(ahead, grid, axis, -1)
        behind = send(behind, grid, axis, 1)
        slots[k], slots[n - k] = ahead, behind
    half = block.shape[1] // 2
    first = send(behind[:, :half], grid, axis, 1)
    second = send(ahead[:, half:], grid, axis, -1)
    return [slots[r] for r in range(n // 2)] + [first, second] + [slots[r] for r in range(n // 2 + 1, n)]


def ring_reduce_pieces(parts, grid, axis):
    n = grid[axis]
    if n % 2 or n < 4:
        return ring_reduce_slots(parts, grid, axis)
    parts = list(parts)
    far_first, far_second = parts[n // 2], parts[n // 2 + 1]
    slots = parts[: n // 2] + [None] + parts[n // 2 + 2:]
    half = far_first.shape[1]
    got_first = send(far_first.astype(jnp.bfloat16), grid, axis, 1).astype(jnp.float32)
    got_second = send(far_second.astype(jnp.bfloat16), grid, axis, -1).astype(jnp.float32)
    top = (n - 1) // 2
    lead, tail = slots[top].astype(jnp.float32), slots[n - top].astype(jnp.float32)
    acc_ahead = jnp.concatenate([lead[:, :half] + got_first, lead[:, half:]], axis=1)
    acc_behind = jnp.concatenate([tail[:, :half], tail[:, half:] + got_second], axis=1)
    for k in range(top, 0, -1):
        got_ahead = send(acc_ahead.astype(jnp.bfloat16), grid, axis, 1).astype(jnp.float32)
        got_behind = send(acc_behind.astype(jnp.bfloat16), grid, axis, -1).astype(jnp.float32)
        if k > 1:
            acc_ahead = slots[k - 1].astype(jnp.float32) + got_ahead
            acc_behind = slots[n - k + 1].astype(jnp.float32) + got_behind
        else:
            return slots[0].astype(jnp.float32) + got_ahead + got_behind


def ring_gather(block, grid, axis):
    n = grid[axis]
    slots = {0: block}
    ahead, behind = block, block
    for k in range(1, (n - 1) // 2 + 1):
        ahead = send(ahead, grid, axis, -1)
        behind = send(behind, grid, axis, 1)
        slots[k], slots[n - k] = ahead, behind
    if n % 2 == 0:
        if n == 2:
            slots[1] = send(block, grid, axis, -1)
        else:
            half = block.shape[1] // 2
            first = send(behind[:, :half], grid, axis, 1)
            second = send(ahead[:, half:], grid, axis, -1)
            slots[n // 2] = jnp.concatenate([first, second], axis=1)
    return jnp.concatenate([slots[r] for r in range(n)], axis=1)


def ring_reduce(parts, grid, axis):
    n = grid[axis]
    rows, total, width = parts.shape
    m = total // n
    slots = [parts[:, r * m:(r + 1) * m].astype(jnp.float32) for r in range(n)]
    if n == 1:
        return slots[0]
    if n == 2:
        return slots[0] + send(slots[1].astype(jnp.bfloat16), grid, axis, 1).astype(jnp.float32)
    top = (n - 1) // 2
    acc_ahead, acc_behind = slots[top], slots[n - top]
    if n % 2 == 0:
        half = m // 2
        far = slots[n // 2].astype(jnp.bfloat16)
        got_first = send(far[:, :half], grid, axis, 1).astype(jnp.float32)
        got_second = send(far[:, half:], grid, axis, -1).astype(jnp.float32)
        acc_ahead = acc_ahead + jnp.concatenate([got_first, jnp.zeros_like(got_first)], axis=1)
        acc_behind = acc_behind + jnp.concatenate([jnp.zeros_like(got_second), got_second], axis=1)
    for k in range(top, 0, -1):
        got_ahead = send(acc_ahead.astype(jnp.bfloat16), grid, axis, 1).astype(jnp.float32)
        got_behind = send(acc_behind.astype(jnp.bfloat16), grid, axis, -1).astype(jnp.float32)
        if k > 1:
            acc_ahead = slots[k - 1] + got_ahead
            acc_behind = slots[n - k + 1] + got_behind
        else:
            return slots[0] + got_ahead + got_behind


def torus_gather(block, grid, order):
    rows, m, width = block.shape
    out = ring_gather(block, grid, order[1])
    return ring_gather(out, grid, order[0])


def torus_reduce(parts, grid, order):
    out = ring_reduce(parts, grid, order[0])
    return ring_reduce(out, grid, order[1])


def on_device(grid, candidates, kv_cache, cache_request, rank_request, hist_blocks, w_uq, w_out):
    groups = lax.axis_size("group")
    per_group = kv_cache.shape[0]
    cand_rows = candidates.shape[0]
    width = candidates.shape[2]
    head_dim = width // HEADS
    count = kv_cache.shape[1]
    capacity = (per_group + groups - 1) // groups
    group_now = lax.axis_index("group")
    member_now = lax.axis_index("member")
    target, arrival, slot_of_pos = routing(cache_request, rank_request, per_group)
    first_slot = group_now * per_group
    local_target = lax.dynamic_slice_in_dim(target, first_slot, per_group)
    local_arrival = lax.dynamic_slice_in_dim(arrival, first_slot, per_group)
    row_index = local_target * capacity + local_arrival
    target_grid = jnp.arange(groups)[:, None, None]
    place_grid = jnp.arange(capacity)[None, :, None]
    hits = (local_target[None, None, :] == target_grid) & (
        local_arrival[None, None, :] == place_grid
    )
    chosen = jnp.sum(jnp.where(hits, jnp.arange(per_group)[None, None, :], 0), axis=2).reshape(-1)
    filled = jnp.any(hits, axis=2).reshape(-1)
    positions = first_slot + jnp.arange(per_group)
    source_slot = slot_of_pos[positions]
    receive_index = source_slot // per_group * capacity + arrival[source_slot]
    send_hits = receive_index[None, :] == jnp.arange(groups * capacity)[:, None]
    send_pos = jnp.sum(jnp.where(send_hits, jnp.arange(per_group)[None, :], 0), axis=1)
    send_filled = jnp.any(send_hits, axis=1)
    row_live = (hist_blocks[cache_request[first_slot + jnp.arange(per_group)]] * BLK).astype(
        jnp.float32
    )

    inputs = candidates.astype(jnp.float32)
    normed = layer_norm(inputs).astype(jnp.bfloat16).reshape(cand_rows * per_group, width)
    queries = jax.nn.silu(jnp.dot(normed, w_uq[:, width:], preferred_element_type=jnp.float32))
    queries = queries.astype(jnp.bfloat16).reshape(cand_rows, per_group, width)
    scale = head_dim ** (-0.5)

    q_pos = jnp.swapaxes(queries, 0, 1)
    q_out = jnp.where(send_filled[:, None, None], q_pos[send_pos], jnp.zeros((), jnp.bfloat16))
    q_in = lax.all_to_all(q_out, "group", split_axis=0, concat_axis=0, tiled=True)
    q_rows = q_in[row_index]
    split = per_group // 2
    halves = ((slice(0, split), (0, 1)), (slice(split, per_group), (1, 0)))
    sums = []
    for rows_of, order in halves:
        inner = ring_gather(q_rows[rows_of], grid, order[1])
        partials = attend_local(
            ring_gather_pieces(inner, grid, order[0]),
            kv_cache[rows_of],
            row_live[rows_of],
            member_now * count,
            scale,
            HEADS,
            jnp.bfloat16,
        )
        outer = ring_reduce_pieces(partials, grid, order[0]).astype(jnp.bfloat16)
        sums.append(ring_reduce(outer, grid, order[1]))
    summed = jnp.concatenate(sums, axis=0).astype(jnp.bfloat16)

    a_out = jnp.where(filled[:, None, None], summed[chosen], jnp.zeros((), summed.dtype))
    a_in = lax.all_to_all(a_out, "group", split_axis=0, concat_axis=0, tiled=True)
    attn = jnp.swapaxes(a_in[receive_index], 0, 1).astype(jnp.float32)

    gates = jax.nn.silu(jnp.dot(normed, w_uq[:, :width], preferred_element_type=jnp.float32))
    gates = gates.reshape(cand_rows, per_group, width)
    gated = (layer_norm(attn) * gates).astype(jnp.bfloat16).reshape(cand_rows * per_group, width)
    result = jnp.dot(gated, w_out, preferred_element_type=jnp.float32) + inputs.reshape(
        cand_rows * per_group, width
    )
    return result.astype(jnp.bfloat16).reshape(cand_rows, per_group, width)


def member_grid(mesh):
    members = mesh.shape["member"]
    try:
        line = mesh.devices[0]
        cols = len({d.coords[0] for d in line})
    except (AttributeError, TypeError, IndexError):
        cols = int(round(members ** 0.5))
    if cols < 1 or members % cols:
        cols = members
    return (members // cols, cols)


def solution(mesh):
    return jax.shard_map(
        functools.partial(on_device, member_grid(mesh)),
        mesh=mesh,
        in_specs=(P("member", "group", None), P("group", "member", None), P(), P(), P(), P(), P()),
        out_specs=P("member", "group", None),
        check_vma=False,
    )
```

```python
import functools

import jax
import jax.numpy as jnp
from jax import lax
from jax.experimental import pallas as pl
from jax.experimental.pallas import tpu as pltpu
from jax.sharding import PartitionSpec as P

HEADS = 8
BLK = 128


def layer_norm(values):
    center = values - jnp.mean(values, axis=-1, keepdims=True)
    spread = jnp.mean(center * center, axis=-1, keepdims=True)
    return center * lax.rsqrt(spread + 1e-05)


def routing(cache_request, rank_request, per_group):
    slot_ids = jnp.arange(cache_request.shape[0], dtype=jnp.int32)
    match = cache_request[:, None] == rank_request[None, :]
    rank_pos = jnp.sum(jnp.where(match, slot_ids[None, :], 0), axis=1)
    target = rank_pos // per_group
    owner_grp = slot_ids // per_group
    earlier = (
        (owner_grp[:, None] == owner_grp[None, :])
        & (target[:, None] == target[None, :])
        & (slot_ids[None, :] < slot_ids[:, None])
    )
    arrival = jnp.sum(earlier.astype(jnp.int32), axis=1)
    slot_of_pos = jnp.sum(jnp.where(match, slot_ids[:, None], 0), axis=0)
    return (target, arrival, slot_of_pos)


def attend_kernel(n_live_ref, q_ref, kt_ref, v_ref, keep_ref, o_ref, *, heads, head_dim, scale):
    row = pl.program_id(0)

    @pl.when(n_live_ref[row] <= 0)
    def _():
        o_ref[...] = jnp.zeros(o_ref.shape, o_ref.dtype)

    @pl.when(n_live_ref[row] > 0)
    def _():
        keep = keep_ref[0]
        for h in range(heads):
            lo = h * head_dim
            q = q_ref[0, :, lo:lo + head_dim]
            kt = kt_ref[0, lo:lo + head_dim, :]
            v = v_ref[0, :, lo:lo + head_dim]
            s = jnp.dot(q, kt, preferred_element_type=jnp.float32)
            w = (jax.nn.silu(s * scale) * keep).astype(jnp.bfloat16)
            o = jnp.dot(w, v, preferred_element_type=jnp.float32)
            o_ref[0, :, lo:lo + head_dim] = o.astype(o_ref.dtype)


def attend_local(queries, piece, live, first_event, scale, heads, out_dtype):
    rows, cands, width = queries.shape
    count = piece.shape[1]
    head_dim = width // heads
    keys_t = jnp.swapaxes(piece[:, :, :width], 1, 2)
    events = (first_event + jnp.arange(count)).astype(jnp.float32)
    keep = ((events[None, :] < live[:, None]).astype(jnp.float32) / live[:, None])[:, None, :]
    n_live = jnp.clip(live.astype(jnp.int32) - first_event, 0, count).astype(jnp.int32)
    kernel = functools.partial(attend_kernel, heads=heads, head_dim=head_dim, scale=scale)
    flops = 4 * rows * cands * count * width
    return pl.pallas_call(
        kernel,
        out_shape=jax.ShapeDtypeStruct((rows, cands, width), out_dtype),
        grid_spec=pltpu.PrefetchScalarGridSpec(
            num_scalar_prefetch=1,
            grid=(rows,),
            in_specs=[
                pl.BlockSpec((1, cands, width), lambda r, n: (r, 0, 0)),
                pl.BlockSpec((1, width, count), lambda r, n: (r, 0, 0)),
                pl.BlockSpec((1, count, width), lambda r, n: (r, 0, 1)),
                pl.BlockSpec((1, 1, count), lambda r, n: (r, 0, 0)),
            ],
            out_specs=pl.BlockSpec((1, cands, width), lambda r, n: (r, 0, 0)),
        ),
        cost_estimate=pl.CostEstimate(
            flops=flops,
            transcendentals=rows * cands * count * heads,
            bytes_accessed=rows * (cands * width * 4 + count * width * 4),
        ),
    )(n_live, queries, keys_t, piece, keep)


def shift_perm(grid, axis, shift):
    rows, cols = grid
    pairs = []
    for zi in range(rows):
        for xi in range(cols):
            if axis == 0:
                dst = ((zi + shift) % rows) * cols + xi
            else:
                dst = zi * cols + (xi + shift) % cols
            pairs.append((zi * cols + xi, dst))
    return pairs


def send(value, grid, axis, shift):
    return lax.ppermute(value, "member", shift_perm(grid, axis, shift))


def ring_gather(block, grid, axis):
    n = grid[axis]
    slots = {0: block}
    ahead, behind = block, block
    for k in range(1, (n - 1) // 2 + 1):
        ahead = send(ahead, grid, axis, -1)
        behind = send(behind, grid, axis, 1)
        slots[k], slots[n - k] = ahead, behind
    if n % 2 == 0:
        if n == 2:
            slots[1] = send(block, grid, axis, -1)
        else:
            half = block.shape[1] // 2
            first = send(behind[:, :half], grid, axis, 1)
            second = send(ahead[:, half:], grid, axis, -1)
            slots[n // 2] = jnp.concatenate([first, second], axis=1)
    return jnp.concatenate([slots[r] for r in range(n)], axis=1)


def ring_reduce(parts, grid, axis):
    n = grid[axis]
    rows, total, width = parts.shape
    m = total // n
    slots = [parts[:, r * m:(r + 1) * m].astype(jnp.float32) for r in range(n)]
    if n == 1:
        return slots[0]
    if n == 2:
        return slots[0] + send(slots[1].astype(jnp.bfloat16), grid, axis, 1).astype(jnp.float32)
    top = (n - 1) // 2
    acc_ahead, acc_behind = slots[top], slots[n - top]
    if n % 2 == 0:
        half = m // 2
        far = slots[n // 2].astype(jnp.bfloat16)
        got_first = send(far[:, :half], grid, axis, 1).astype(jnp.float32)
        got_second = send(far[:, half:], grid, axis, -1).astype(jnp.float32)
        acc_ahead = acc_ahead + jnp.concatenate([got_first, jnp.zeros_like(got_first)], axis=1)
        acc_behind = acc_behind + jnp.concatenate([jnp.zeros_like(got_second), got_second], axis=1)
    for k in range(top, 0, -1):
        got_ahead = send(acc_ahead.astype(jnp.bfloat16), grid, axis, 1).astype(jnp.float32)
        got_behind = send(acc_behind.astype(jnp.bfloat16), grid, axis, -1).astype(jnp.float32)
        if k > 1:
            acc_ahead = slots[k - 1] + got_ahead
            acc_behind = slots[n - k + 1] + got_behind
        else:
            return slots[0] + got_ahead + got_behind


def torus_gather(block, grid, order):
    rows, m, width = block.shape
    out = ring_gather(block, grid, order[1])
    return ring_gather(out, grid, order[0])


def torus_reduce(parts, grid, order):
    out = ring_reduce(parts, grid, order[0])
    return ring_reduce(out, grid, order[1])


def on_device(grid, candidates, kv_cache, cache_request, rank_request, hist_blocks, w_uq, w_out):
    groups = lax.axis_size("group")
    per_group = kv_cache.shape[0]
    cand_rows = candidates.shape[0]
    width = candidates.shape[2]
    head_dim = width // HEADS
    count = kv_cache.shape[1]
    capacity = (per_group + groups - 1) // groups
    group_now = lax.axis_index("group")
    member_now = lax.axis_index("member")
    target, arrival, slot_of_pos = routing(cache_request, rank_request, per_group)
    first_slot = group_now * per_group
    local_target = lax.dynamic_slice_in_dim(target, first_slot, per_group)
    local_arrival = lax.dynamic_slice_in_dim(arrival, first_slot, per_group)
    row_index = local_target * capacity + local_arrival
    target_grid = jnp.arange(groups)[:, None, None]
    place_grid = jnp.arange(capacity)[None, :, None]
    hits = (local_target[None, None, :] == target_grid) & (
        local_arrival[None, None, :] == place_grid
    )
    chosen = jnp.sum(jnp.where(hits, jnp.arange(per_group)[None, None, :], 0), axis=2).reshape(-1)
    filled = jnp.any(hits, axis=2).reshape(-1)
    positions = first_slot + jnp.arange(per_group)
    source_slot = slot_of_pos[positions]
    receive_index = source_slot // per_group * capacity + arrival[source_slot]
    send_hits = receive_index[None, :] == jnp.arange(groups * capacity)[:, None]
    send_pos = jnp.sum(jnp.where(send_hits, jnp.arange(per_group)[None, :], 0), axis=1)
    send_filled = jnp.any(send_hits, axis=1)
    row_live = (hist_blocks[cache_request[first_slot + jnp.arange(per_group)]] * BLK).astype(
        jnp.float32
    )

    inputs = candidates.astype(jnp.float32)
    normed = layer_norm(inputs).astype(jnp.bfloat16).reshape(cand_rows * per_group, width)
    projected = jax.nn.silu(jnp.dot(normed, w_uq, preferred_element_type=jnp.float32))
    gates = projected[:, :width].reshape(cand_rows, per_group, width)
    queries = projected[:, width:].astype(jnp.bfloat16).reshape(cand_rows, per_group, width)
    scale = head_dim ** (-0.5)

    q_pos = jnp.swapaxes(queries, 0, 1)
    q_out = jnp.where(send_filled[:, None, None], q_pos[send_pos], jnp.zeros((), jnp.bfloat16))
    q_in = lax.all_to_all(q_out, "group", split_axis=0, concat_axis=0, tiled=True)
    q_rows = q_in[row_index]
    split = per_group // 2
    halves = ((slice(0, split), (0, 1)), (slice(split, per_group), (1, 0)))
    sums = []
    for rows_of, order in halves:
        q_all = torus_gather(q_rows[rows_of], grid, order)
        partial = attend_local(
            q_all, kv_cache[rows_of], row_live[rows_of], member_now * count, scale, HEADS, jnp.bfloat16
        )
        sums.append(torus_reduce(partial, grid, order))
    summed = jnp.concatenate(sums, axis=0).astype(jnp.bfloat16)

    a_out = jnp.where(filled[:, None, None], summed[chosen], jnp.zeros((), summed.dtype))
    a_in = lax.all_to_all(a_out, "group", split_axis=0, concat_axis=0, tiled=True)
    attn = jnp.swapaxes(a_in[receive_index], 0, 1).astype(jnp.float32)

    gated = (layer_norm(attn) * gates).astype(jnp.bfloat16).reshape(cand_rows * per_group, width)
    result = jnp.dot(gated, w_out, preferred_element_type=jnp.float32) + inputs.reshape(
        cand_rows * per_group, width
    )
    return result.astype(jnp.bfloat16).reshape(cand_rows, per_group, width)


def member_grid(mesh):
    members = mesh.shape["member"]
    try:
        line = mesh.devices[0]
        cols = len({d.coords[0] for d in line})
    except (AttributeError, TypeError, IndexError):
        cols = int(round(members ** 0.5))
    if cols < 1 or members % cols:
        cols = members
    return (members // cols, cols)


def solution(mesh):
    return jax.shard_map(
        functools.partial(on_device, member_grid(mesh)),
        mesh=mesh,
        in_specs=(P("member", "group", None), P("group", "member", None), P(), P(), P(), P(), P()),
        out_specs=P("member", "group", None),
        check_vma=False,
    )
```

```python
import functools

import jax
import jax.numpy as jnp
from jax import lax
from jax.experimental import pallas as pl
from jax.experimental.pallas import tpu as pltpu
from jax.sharding import PartitionSpec as P

HEADS = 8
BLK = 128


def layer_norm(values):
    center = values - jnp.mean(values, axis=-1, keepdims=True)
    spread = jnp.mean(center * center, axis=-1, keepdims=True)
    return center * lax.rsqrt(spread + 1e-05)


def routing(cache_request, rank_request, per_group):
    slot_ids = jnp.arange(cache_request.shape[0], dtype=jnp.int32)
    match = cache_request[:, None] == rank_request[None, :]
    rank_pos = jnp.sum(jnp.where(match, slot_ids[None, :], 0), axis=1)
    target = rank_pos // per_group
    owner_grp = slot_ids // per_group
    earlier = (
        (owner_grp[:, None] == owner_grp[None, :])
        & (target[:, None] == target[None, :])
        & (slot_ids[None, :] < slot_ids[:, None])
    )
    arrival = jnp.sum(earlier.astype(jnp.int32), axis=1)
    slot_of_pos = jnp.sum(jnp.where(match, slot_ids[:, None], 0), axis=0)
    return (target, arrival, slot_of_pos)


def attend_kernel(n_live_ref, q_ref, kv_ref, keep_ref, o_ref, *, heads, head_dim, scale):
    row = pl.program_id(0)
    width = heads * head_dim

    @pl.when(n_live_ref[row] <= 0)
    def _():
        o_ref[...] = jnp.zeros(o_ref.shape, o_ref.dtype)

    @pl.when(n_live_ref[row] > 0)
    def _():
        half_keep = keep_ref[0] * 0.5
        for h in range(heads):
            lo = h * head_dim
            q = q_ref[0, :, lo:lo + head_dim]
            k = kv_ref[0, :, lo:lo + head_dim]
            v = kv_ref[0, :, width + lo:width + lo + head_dim]
            s = lax.dot_general(q, k, (((1,), (1,)), ((), ())), preferred_element_type=jnp.float32)
            y = s * scale
            w = (y * (1.0 + jnp.tanh(y * 0.5)) * half_keep).astype(jnp.bfloat16)
            o = jnp.dot(w, v, preferred_element_type=jnp.float32)
            o_ref[0, :, lo:lo + head_dim] = o.astype(o_ref.dtype)


def attend_local(queries, piece, live, first_event, scale, heads, out_dtype):
    rows, cands, width = queries.shape
    count = piece.shape[1]
    head_dim = width // heads
    events = (first_event + jnp.arange(count)).astype(jnp.float32)
    keep = ((events[None, :] < live[:, None]).astype(jnp.float32) / live[:, None])[:, None, :]
    n_live = jnp.clip(live.astype(jnp.int32) - first_event, 0, count).astype(jnp.int32)
    kernel = functools.partial(attend_kernel, heads=heads, head_dim=head_dim, scale=scale)
    flops = 4 * rows * cands * count * width
    return pl.pallas_call(
        kernel,
        out_shape=jax.ShapeDtypeStruct((rows, cands, width), out_dtype),
        grid_spec=pltpu.PrefetchScalarGridSpec(
            num_scalar_prefetch=1,
            grid=(rows,),
            in_specs=[
                pl.BlockSpec((1, cands, width), lambda r, n: (r, 0, 0)),
                pl.BlockSpec((1, count, 2 * width), lambda r, n: (r, 0, 0)),
                pl.BlockSpec((1, 1, count), lambda r, n: (r, 0, 0)),
            ],
            out_specs=pl.BlockSpec((1, cands, width), lambda r, n: (r, 0, 0)),
        ),
        cost_estimate=pl.CostEstimate(
            flops=flops,
            transcendentals=rows * cands * count * heads,
            bytes_accessed=rows * (cands * width * 4 + count * width * 4),
        ),
    )(n_live, queries, piece, keep)


def shift_perm(grid, axis, shift):
    rows, cols = grid
    pairs = []
    for zi in range(rows):
        for xi in range(cols):
            if axis == 0:
                dst = ((zi + shift) % rows) * cols + xi
            else:
                dst = zi * cols + (xi + shift) % cols
            pairs.append((zi * cols + xi, dst))
    return pairs


def send(value, grid, axis, shift):
    return lax.ppermute(value, "member", shift_perm(grid, axis, shift))


def ring_gather(block, grid, axis):
    n = grid[axis]
    slots = {0: block}
    ahead, behind = block, block
    for k in range(1, (n - 1) // 2 + 1):
        ahead = send(ahead, grid, axis, -1)
        behind = send(behind, grid, axis, 1)
        slots[k], slots[n - k] = ahead, behind
    if n % 2 == 0:
        if n == 2:
            slots[1] = send(block, grid, axis, -1)
        else:
            half = block.shape[1] // 2
            first = send(behind[:, :half], grid, axis, 1)
            second = send(ahead[:, half:], grid, axis, -1)
            slots[n // 2] = jnp.concatenate([first, second], axis=1)
    return jnp.concatenate([slots[r] for r in range(n)], axis=1)


def ring_reduce(parts, grid, axis):
    n = grid[axis]
    rows, total, width = parts.shape
    m = total // n
    slots = [parts[:, r * m:(r + 1) * m].astype(jnp.float32) for r in range(n)]
    if n == 1:
        return slots[0]
    if n == 2:
        return slots[0] + send(slots[1].astype(jnp.bfloat16), grid, axis, 1).astype(jnp.float32)
    top = (n - 1) // 2
    acc_ahead, acc_behind = slots[top], slots[n - top]
    if n % 2 == 0:
        half = m // 2
        far = slots[n // 2].astype(jnp.bfloat16)
        got_first = send(far[:, :half], grid, axis, 1).astype(jnp.float32)
        got_second = send(far[:, half:], grid, axis, -1).astype(jnp.float32)
        acc_ahead = acc_ahead + jnp.concatenate([got_first, jnp.zeros_like(got_first)], axis=1)
        acc_behind = acc_behind + jnp.concatenate([jnp.zeros_like(got_second), got_second], axis=1)
    for k in range(top, 0, -1):
        got_ahead = send(acc_ahead.astype(jnp.bfloat16), grid, axis, 1).astype(jnp.float32)
        got_behind = send(acc_behind.astype(jnp.bfloat16), grid, axis, -1).astype(jnp.float32)
        if k > 1:
            acc_ahead = slots[k - 1] + got_ahead
            acc_behind = slots[n - k + 1] + got_behind
        else:
            return slots[0] + got_ahead + got_behind


def torus_gather(block, grid, order):
    rows, m, width = block.shape
    out = ring_gather(block, grid, order[1])
    return ring_gather(out, grid, order[0])


def torus_reduce(parts, grid, order):
    out = ring_reduce(parts, grid, order[0])
    return ring_reduce(out, grid, order[1])


def on_device(grid, candidates, kv_cache, cache_request, rank_request, hist_blocks, w_uq, w_out):
    groups = lax.axis_size("group")
    per_group = kv_cache.shape[0]
    cand_rows = candidates.shape[0]
    width = candidates.shape[2]
    head_dim = width // HEADS
    count = kv_cache.shape[1]
    capacity = (per_group + groups - 1) // groups
    group_now = lax.axis_index("group")
    member_now = lax.axis_index("member")
    target, arrival, slot_of_pos = routing(cache_request, rank_request, per_group)
    first_slot = group_now * per_group
    local_target = lax.dynamic_slice_in_dim(target, first_slot, per_group)
    local_arrival = lax.dynamic_slice_in_dim(arrival, first_slot, per_group)
    row_index = local_target * capacity + local_arrival
    target_grid = jnp.arange(groups)[:, None, None]
    place_grid = jnp.arange(capacity)[None, :, None]
    hits = (local_target[None, None, :] == target_grid) & (
        local_arrival[None, None, :] == place_grid
    )
    chosen = jnp.sum(jnp.where(hits, jnp.arange(per_group)[None, None, :], 0), axis=2).reshape(-1)
    filled = jnp.any(hits, axis=2).reshape(-1)
    positions = first_slot + jnp.arange(per_group)
    source_slot = slot_of_pos[positions]
    receive_index = source_slot // per_group * capacity + arrival[source_slot]
    send_hits = receive_index[None, :] == jnp.arange(groups * capacity)[:, None]
    send_pos = jnp.sum(jnp.where(send_hits, jnp.arange(per_group)[None, :], 0), axis=1)
    send_filled = jnp.any(send_hits, axis=1)
    row_live = (hist_blocks[cache_request[first_slot + jnp.arange(per_group)]] * BLK).astype(
        jnp.float32
    )

    inputs = candidates.astype(jnp.float32)
    normed = layer_norm(inputs).astype(jnp.bfloat16).reshape(cand_rows * per_group, width)
    queries = jax.nn.silu(jnp.dot(normed, w_uq[:, width:], preferred_element_type=jnp.float32))
    queries = queries.astype(jnp.bfloat16).reshape(cand_rows, per_group, width)
    scale = head_dim ** (-0.5)

    q_pos = jnp.swapaxes(queries, 0, 1)
    q_out = jnp.where(send_filled[:, None, None], q_pos[send_pos], jnp.zeros((), jnp.bfloat16))
    q_in = lax.all_to_all(q_out, "group", split_axis=0, concat_axis=0, tiled=True)
    q_rows = q_in[row_index]
    split = per_group // 2
    halves = ((slice(0, split), (0, 1)), (slice(split, per_group), (1, 0)))
    sums = []
    for rows_of, order in halves:
        q_all = torus_gather(q_rows[rows_of], grid, order)
        partial = attend_local(
            q_all, kv_cache[rows_of], row_live[rows_of], member_now * count, scale, HEADS, jnp.bfloat16
        )
        sums.append(torus_reduce(partial, grid, order))
    summed = jnp.concatenate(sums, axis=0).astype(jnp.bfloat16)

    a_out = jnp.where(filled[:, None, None], summed[chosen], jnp.zeros((), summed.dtype))
    a_in = lax.all_to_all(a_out, "group", split_axis=0, concat_axis=0, tiled=True)
    attn = jnp.swapaxes(a_in[receive_index], 0, 1).astype(jnp.float32)

    gates = jax.nn.silu(jnp.dot(normed, w_uq[:, :width], preferred_element_type=jnp.float32))
    gates = gates.reshape(cand_rows, per_group, width)
    gated = (layer_norm(attn) * gates).astype(jnp.bfloat16).reshape(cand_rows * per_group, width)
    result = jnp.dot(gated, w_out, preferred_element_type=jnp.float32) + inputs.reshape(
        cand_rows * per_group, width
    )
    return result.astype(jnp.bfloat16).reshape(cand_rows, per_group, width)


def member_grid(mesh):
    members = mesh.shape["member"]
    try:
        line = mesh.devices[0]
        cols = len({d.coords[0] for d in line})
    except (AttributeError, TypeError, IndexError):
        cols = int(round(members ** 0.5))
    if cols < 1 or members % cols:
        cols = members
    return (members // cols, cols)


def solution(mesh):
    return jax.shard_map(
        functools.partial(on_device, member_grid(mesh)),
        mesh=mesh,
        in_specs=(P("member", "group", None), P("group", "member", None), P(), P(), P(), P(), P()),
        out_specs=P("member", "group", None),
        check_vma=False,
    )
```

```python
import functools

import jax
import jax.numpy as jnp
from jax import lax
from jax.experimental import pallas as pl
from jax.experimental.pallas import tpu as pltpu
from jax.sharding import PartitionSpec as P

HEADS = 8
BLK = 128


def layer_norm(values):
    center = values - jnp.mean(values, axis=-1, keepdims=True)
    spread = jnp.mean(center * center, axis=-1, keepdims=True)
    return center * lax.rsqrt(spread + 1e-05)


def routing(cache_request, rank_request, per_group):
    slot_ids = jnp.arange(cache_request.shape[0], dtype=jnp.int32)
    match = cache_request[:, None] == rank_request[None, :]
    rank_pos = jnp.sum(jnp.where(match, slot_ids[None, :], 0), axis=1)
    target = rank_pos // per_group
    owner_grp = slot_ids // per_group
    earlier = (
        (owner_grp[:, None] == owner_grp[None, :])
        & (target[:, None] == target[None, :])
        & (slot_ids[None, :] < slot_ids[:, None])
    )
    arrival = jnp.sum(earlier.astype(jnp.int32), axis=1)
    slot_of_pos = jnp.sum(jnp.where(match, slot_ids[:, None], 0), axis=0)
    return (target, arrival, slot_of_pos)


def attend_kernel(n_live_ref, q_ref, kv_ref, vk_ref, o_ref, *, heads, head_dim):
    row = pl.program_id(0)

    @pl.when(n_live_ref[row] <= 0)
    def _():
        o_ref[...] = jnp.zeros(o_ref.shape, o_ref.dtype)

    @pl.when(n_live_ref[row] > 0)
    def _():
        for h in range(heads):
            lo = h * head_dim
            q = q_ref[0, :, lo:lo + head_dim]
            k = kv_ref[0, :, lo:lo + head_dim]
            v = vk_ref[0, :, lo:lo + head_dim]
            t = lax.dot_general(q, k, (((1,), (1,)), ((), ())), preferred_element_type=jnp.float32)
            w = (t * (1.0 + jnp.tanh(t))).astype(jnp.bfloat16)
            o = jnp.dot(w, v, preferred_element_type=jnp.float32)
            o_ref[0, :, lo:lo + head_dim] = o.astype(o_ref.dtype)


def attend_local(queries, piece, live, first_event, heads, out_dtype):
    rows, cands, width = queries.shape
    count = piece.shape[1]
    head_dim = width // heads
    events = (first_event + jnp.arange(count)).astype(jnp.float32)
    keep = (events[None, :] < live[:, None]).astype(jnp.float32) / live[:, None]
    values = (piece[:, :, width:].astype(jnp.float32) * keep[:, :, None]).astype(jnp.bfloat16)
    n_live = jnp.clip(live.astype(jnp.int32) - first_event, 0, count).astype(jnp.int32)
    kernel = functools.partial(attend_kernel, heads=heads, head_dim=head_dim)
    flops = 4 * rows * cands * count * width
    return pl.pallas_call(
        kernel,
        out_shape=jax.ShapeDtypeStruct((rows, cands, width), out_dtype),
        grid_spec=pltpu.PrefetchScalarGridSpec(
            num_scalar_prefetch=1,
            grid=(rows,),
            in_specs=[
                pl.BlockSpec((1, cands, width), lambda r, n: (r, 0, 0)),
                pl.BlockSpec((1, count, width), lambda r, n: (r, 0, 0)),
                pl.BlockSpec((1, count, width), lambda r, n: (r, 0, 0)),
            ],
            out_specs=pl.BlockSpec((1, cands, width), lambda r, n: (r, 0, 0)),
        ),
        cost_estimate=pl.CostEstimate(
            flops=flops,
            transcendentals=rows * cands * count * heads,
            bytes_accessed=rows * (cands * width * 4 + count * width * 4),
        ),
    )(n_live, queries, piece, values)


def shift_perm(grid, axis, shift):
    rows, cols = grid
    pairs = []
    for zi in range(rows):
        for xi in range(cols):
            if axis == 0:
                dst = ((zi + shift) % rows) * cols + xi
            else:
                dst = zi * cols + (xi + shift) % cols
            pairs.append((zi * cols + xi, dst))
    return pairs


def send(value, grid, axis, shift):
    return lax.ppermute(value, "member", shift_perm(grid, axis, shift))


def ring_gather(block, grid, axis):
    n = grid[axis]
    slots = {0: block}
    ahead, behind = block, block
    for k in range(1, (n - 1) // 2 + 1):
        ahead = send(ahead, grid, axis, -1)
        behind = send(behind, grid, axis, 1)
        slots[k], slots[n - k] = ahead, behind
    if n % 2 == 0:
        if n == 2:
            slots[1] = send(block, grid, axis, -1)
        else:
            half = block.shape[1] // 2
            first = send(behind[:, :half], grid, axis, 1)
            second = send(ahead[:, half:], grid, axis, -1)
            slots[n // 2] = jnp.concatenate([first, second], axis=1)
    return jnp.concatenate([slots[r] for r in range(n)], axis=1)


def ring_reduce(parts, grid, axis):
    n = grid[axis]
    rows, total, width = parts.shape
    m = total // n
    slots = [parts[:, r * m:(r + 1) * m].astype(jnp.float32) for r in range(n)]
    if n == 1:
        return slots[0]
    if n == 2:
        return slots[0] + send(slots[1].astype(jnp.bfloat16), grid, axis, 1).astype(jnp.float32)
    top = (n - 1) // 2
    acc_ahead, acc_behind = slots[top], slots[n - top]
    if n % 2 == 0:
        half = m // 2
        far = slots[n // 2].astype(jnp.bfloat16)
        got_first = send(far[:, :half], grid, axis, 1).astype(jnp.float32)
        got_second = send(far[:, half:], grid, axis, -1).astype(jnp.float32)
        acc_ahead = acc_ahead + jnp.concatenate([got_first, jnp.zeros_like(got_first)], axis=1)
        acc_behind = acc_behind + jnp.concatenate([jnp.zeros_like(got_second), got_second], axis=1)
    for k in range(top, 0, -1):
        got_ahead = send(acc_ahead.astype(jnp.bfloat16), grid, axis, 1).astype(jnp.float32)
        got_behind = send(acc_behind.astype(jnp.bfloat16), grid, axis, -1).astype(jnp.float32)
        if k > 1:
            acc_ahead = slots[k - 1] + got_ahead
            acc_behind = slots[n - k + 1] + got_behind
        else:
            return slots[0] + got_ahead + got_behind


def torus_gather(block, grid, order):
    rows, m, width = block.shape
    out = ring_gather(block, grid, order[1])
    return ring_gather(out, grid, order[0])


def torus_reduce(parts, grid, order):
    out = ring_reduce(parts, grid, order[0])
    return ring_reduce(out, grid, order[1])


def on_device(grid, candidates, kv_cache, cache_request, rank_request, hist_blocks, w_uq, w_out):
    groups = lax.axis_size("group")
    per_group = kv_cache.shape[0]
    cand_rows = candidates.shape[0]
    width = candidates.shape[2]
    head_dim = width // HEADS
    count = kv_cache.shape[1]
    capacity = (per_group + groups - 1) // groups
    group_now = lax.axis_index("group")
    member_now = lax.axis_index("member")
    target, arrival, slot_of_pos = routing(cache_request, rank_request, per_group)
    first_slot = group_now * per_group
    local_target = lax.dynamic_slice_in_dim(target, first_slot, per_group)
    local_arrival = lax.dynamic_slice_in_dim(arrival, first_slot, per_group)
    row_index = local_target * capacity + local_arrival
    target_grid = jnp.arange(groups)[:, None, None]
    place_grid = jnp.arange(capacity)[None, :, None]
    hits = (local_target[None, None, :] == target_grid) & (
        local_arrival[None, None, :] == place_grid
    )
    chosen = jnp.sum(jnp.where(hits, jnp.arange(per_group)[None, None, :], 0), axis=2).reshape(-1)
    filled = jnp.any(hits, axis=2).reshape(-1)
    positions = first_slot + jnp.arange(per_group)
    source_slot = slot_of_pos[positions]
    receive_index = source_slot // per_group * capacity + arrival[source_slot]
    send_hits = receive_index[None, :] == jnp.arange(groups * capacity)[:, None]
    send_pos = jnp.sum(jnp.where(send_hits, jnp.arange(per_group)[None, :], 0), axis=1)
    send_filled = jnp.any(send_hits, axis=1)
    row_live = (hist_blocks[cache_request[first_slot + jnp.arange(per_group)]] * BLK).astype(
        jnp.float32
    )

    inputs = candidates.astype(jnp.float32)
    normed = layer_norm(inputs).astype(jnp.bfloat16).reshape(cand_rows * per_group, width)
    queries = jax.nn.silu(jnp.dot(normed, w_uq[:, width:], preferred_element_type=jnp.float32))
    queries = (queries * (0.5 * head_dim ** (-0.5))).astype(jnp.bfloat16).reshape(cand_rows, per_group, width)

    q_pos = jnp.swapaxes(queries, 0, 1)
    q_out = jnp.where(send_filled[:, None, None], q_pos[send_pos], jnp.zeros((), jnp.bfloat16))
    q_in = lax.all_to_all(q_out, "group", split_axis=0, concat_axis=0, tiled=True)
    q_rows = q_in[row_index]
    split = per_group // 2
    halves = ((slice(0, split), (0, 1)), (slice(split, per_group), (1, 0)))
    sums = []
    for rows_of, order in halves:
        q_all = torus_gather(q_rows[rows_of], grid, order)
        partial = attend_local(
            q_all, kv_cache[rows_of], row_live[rows_of], member_now * count, HEADS, jnp.bfloat16
        )
        sums.append(torus_reduce(partial, grid, order))
    summed = jnp.concatenate(sums, axis=0).astype(jnp.bfloat16)

    a_out = jnp.where(filled[:, None, None], summed[chosen], jnp.zeros((), summed.dtype))
    a_in = lax.all_to_all(a_out, "group", split_axis=0, concat_axis=0, tiled=True)
    attn = jnp.swapaxes(a_in[receive_index], 0, 1).astype(jnp.float32)

    gates = jax.nn.silu(jnp.dot(normed, w_uq[:, :width], preferred_element_type=jnp.float32))
    gates = gates.reshape(cand_rows, per_group, width)
    gated = (layer_norm(attn) * gates).astype(jnp.bfloat16).reshape(cand_rows * per_group, width)
    result = jnp.dot(gated, w_out, preferred_element_type=jnp.float32) + inputs.reshape(
        cand_rows * per_group, width
    )
    return result.astype(jnp.bfloat16).reshape(cand_rows, per_group, width)


def member_grid(mesh):
    members = mesh.shape["member"]
    try:
        line = mesh.devices[0]
        cols = len({d.coords[0] for d in line})
    except (AttributeError, TypeError, IndexError):
        cols = int(round(members ** 0.5))
    if cols < 1 or members % cols:
        cols = members
    return (members // cols, cols)


def solution(mesh):
    return jax.shard_map(
        functools.partial(on_device, member_grid(mesh)),
        mesh=mesh,
        in_specs=(P("member", "group", None), P("group", "member", None), P(), P(), P(), P(), P()),
        out_specs=P("member", "group", None),
        check_vma=False,
    )
```

```python
import functools

import jax
import jax.numpy as jnp
from jax import lax
from jax.experimental import pallas as pl
from jax.experimental.pallas import tpu as pltpu
from jax.sharding import PartitionSpec as P

HEADS = 8
BLK = 128


def layer_norm(values):
    center = values - jnp.mean(values, axis=-1, keepdims=True)
    spread = jnp.mean(center * center, axis=-1, keepdims=True)
    return center * lax.rsqrt(spread + 1e-05)


def routing(cache_request, rank_request, per_group):
    slot_ids = jnp.arange(cache_request.shape[0], dtype=jnp.int32)
    match = cache_request[:, None] == rank_request[None, :]
    rank_pos = jnp.sum(jnp.where(match, slot_ids[None, :], 0), axis=1)
    target = rank_pos // per_group
    owner_grp = slot_ids // per_group
    earlier = (
        (owner_grp[:, None] == owner_grp[None, :])
        & (target[:, None] == target[None, :])
        & (slot_ids[None, :] < slot_ids[:, None])
    )
    arrival = jnp.sum(earlier.astype(jnp.int32), axis=1)
    slot_of_pos = jnp.sum(jnp.where(match, slot_ids[:, None], 0), axis=0)
    return (target, arrival, slot_of_pos)


def attend_kernel(n_live_ref, q_ref, kv_ref, vk_ref, o_ref, *, heads, head_dim):
    row = pl.program_id(0)

    @pl.when(n_live_ref[row] <= 0)
    def _():
        o_ref[...] = jnp.zeros(o_ref.shape, o_ref.dtype)

    @pl.when(n_live_ref[row] > 0)
    def _():
        for h in range(heads):
            lo = h * head_dim
            q = q_ref[0, :, lo:lo + head_dim]
            k = kv_ref[0, :, lo:lo + head_dim]
            v = vk_ref[0, :, lo:lo + head_dim]
            t = lax.dot_general(q, k, (((1,), (1,)), ((), ())), preferred_element_type=jnp.float32)
            w = (t * (1.0 + jnp.tanh(t))).astype(jnp.bfloat16)
            o = jnp.dot(w, v, preferred_element_type=jnp.float32)
            o_ref[0, :, lo:lo + head_dim] = o.astype(o_ref.dtype)


def attend_local(queries, piece, live, first_event, heads, out_dtype):
    rows, cands, width = queries.shape
    count = piece.shape[1]
    head_dim = width // heads
    events = (first_event + jnp.arange(count)).astype(jnp.float32)
    keep = (events[None, :] < live[:, None]).astype(jnp.float32) / live[:, None]
    values = (piece[:, :, width:].astype(jnp.float32) * keep[:, :, None]).astype(jnp.bfloat16)
    n_live = jnp.clip(live.astype(jnp.int32) - first_event, 0, count).astype(jnp.int32)
    kernel = functools.partial(attend_kernel, heads=heads, head_dim=head_dim)
    flops = 4 * rows * cands * count * width
    return pl.pallas_call(
        kernel,
        out_shape=jax.ShapeDtypeStruct((rows, cands, width), out_dtype),
        grid_spec=pltpu.PrefetchScalarGridSpec(
            num_scalar_prefetch=1,
            grid=(rows,),
            in_specs=[
                pl.BlockSpec((1, cands, width), lambda r, n: (r, 0, 0)),
                pl.BlockSpec((1, count, width), lambda r, n: (r, 0, 0)),
                pl.BlockSpec((1, count, width), lambda r, n: (r, 0, 0)),
            ],
            out_specs=pl.BlockSpec((1, cands, width), lambda r, n: (r, 0, 0)),
        ),
        cost_estimate=pl.CostEstimate(
            flops=flops,
            transcendentals=rows * cands * count * heads,
            bytes_accessed=rows * (cands * width * 4 + count * width * 4),
        ),
    )(n_live, queries, piece, values)


def shift_perm(grid, axis, shift):
    rows, cols = grid
    pairs = []
    for zi in range(rows):
        for xi in range(cols):
            if axis == 0:
                dst = ((zi + shift) % rows) * cols + xi
            else:
                dst = zi * cols + (xi + shift) % cols
            pairs.append((zi * cols + xi, dst))
    return pairs


def send(value, grid, axis, shift):
    return lax.ppermute(value, "member", shift_perm(grid, axis, shift))


def direct_gather(block, grid, axis):
    n = grid[axis]
    return jnp.concatenate([block] + [send(block, grid, axis, -k) for k in range(1, n)], axis=1)


def direct_reduce(parts, grid, axis):
    n = grid[axis]
    m = parts.shape[1] // n
    out = parts[:, :m].astype(jnp.float32)
    for k in range(1, n):
        out = out + send(parts[:, k * m:(k + 1) * m].astype(jnp.bfloat16), grid, axis, k).astype(jnp.float32)
    return out


def ring_gather(block, grid, axis):
    n = grid[axis]
    slots = {0: block}
    ahead, behind = block, block
    for k in range(1, (n - 1) // 2 + 1):
        ahead = send(ahead, grid, axis, -1)
        behind = send(behind, grid, axis, 1)
        slots[k], slots[n - k] = ahead, behind
    if n % 2 == 0:
        if n == 2:
            slots[1] = send(block, grid, axis, -1)
        else:
            half = block.shape[1] // 2
            first = send(behind[:, :half], grid, axis, 1)
            second = send(ahead[:, half:], grid, axis, -1)
            slots[n // 2] = jnp.concatenate([first, second], axis=1)
    return jnp.concatenate([slots[r] for r in range(n)], axis=1)


def ring_reduce(parts, grid, axis):
    n = grid[axis]
    rows, total, width = parts.shape
    m = total // n
    slots = [parts[:, r * m:(r + 1) * m].astype(jnp.float32) for r in range(n)]
    if n == 1:
        return slots[0]
    if n == 2:
        return slots[0] + send(slots[1].astype(jnp.bfloat16), grid, axis, 1).astype(jnp.float32)
    top = (n - 1) // 2
    acc_ahead, acc_behind = slots[top], slots[n - top]
    if n % 2 == 0:
        half = m // 2
        far = slots[n // 2].astype(jnp.bfloat16)
        got_first = send(far[:, :half], grid, axis, 1).astype(jnp.float32)
        got_second = send(far[:, half:], grid, axis, -1).astype(jnp.float32)
        acc_ahead = acc_ahead + jnp.concatenate([got_first, jnp.zeros_like(got_first)], axis=1)
        acc_behind = acc_behind + jnp.concatenate([jnp.zeros_like(got_second), got_second], axis=1)
    for k in range(top, 0, -1):
        got_ahead = send(acc_ahead.astype(jnp.bfloat16), grid, axis, 1).astype(jnp.float32)
        got_behind = send(acc_behind.astype(jnp.bfloat16), grid, axis, -1).astype(jnp.float32)
        if k > 1:
            acc_ahead = slots[k - 1] + got_ahead
            acc_behind = slots[n - k + 1] + got_behind
        else:
            return slots[0] + got_ahead + got_behind


def torus_gather(block, grid, order):
    rows, m, width = block.shape
    out = direct_gather(block, grid, order[1])
    return ring_gather(out, grid, order[0])


def torus_reduce(parts, grid, order):
    out = ring_reduce(parts, grid, order[0]).astype(jnp.bfloat16)
    return direct_reduce(out, grid, order[1])


def on_device(grid, candidates, kv_cache, cache_request, rank_request, hist_blocks, w_uq, w_out):
    groups = lax.axis_size("group")
    per_group = kv_cache.shape[0]
    cand_rows = candidates.shape[0]
    width = candidates.shape[2]
    head_dim = width // HEADS
    count = kv_cache.shape[1]
    capacity = (per_group + groups - 1) // groups
    group_now = lax.axis_index("group")
    member_now = lax.axis_index("member")
    target, arrival, slot_of_pos = routing(cache_request, rank_request, per_group)
    first_slot = group_now * per_group
    local_target = lax.dynamic_slice_in_dim(target, first_slot, per_group)
    local_arrival = lax.dynamic_slice_in_dim(arrival, first_slot, per_group)
    row_index = local_target * capacity + local_arrival
    target_grid = jnp.arange(groups)[:, None, None]
    place_grid = jnp.arange(capacity)[None, :, None]
    hits = (local_target[None, None, :] == target_grid) & (
        local_arrival[None, None, :] == place_grid
    )
    chosen = jnp.sum(jnp.where(hits, jnp.arange(per_group)[None, None, :], 0), axis=2).reshape(-1)
    filled = jnp.any(hits, axis=2).reshape(-1)
    positions = first_slot + jnp.arange(per_group)
    source_slot = slot_of_pos[positions]
    receive_index = source_slot // per_group * capacity + arrival[source_slot]
    send_hits = receive_index[None, :] == jnp.arange(groups * capacity)[:, None]
    send_pos = jnp.sum(jnp.where(send_hits, jnp.arange(per_group)[None, :], 0), axis=1)
    send_filled = jnp.any(send_hits, axis=1)
    row_live = (hist_blocks[cache_request[first_slot + jnp.arange(per_group)]] * BLK).astype(
        jnp.float32
    )

    inputs = candidates.astype(jnp.float32)
    normed = layer_norm(inputs).astype(jnp.bfloat16).reshape(cand_rows * per_group, width)
    queries = jax.nn.silu(jnp.dot(normed, w_uq[:, width:], preferred_element_type=jnp.float32))
    queries = (queries * (0.5 * head_dim ** (-0.5))).astype(jnp.bfloat16).reshape(cand_rows, per_group, width)

    q_pos = jnp.swapaxes(queries, 0, 1)
    q_out = jnp.where(send_filled[:, None, None], q_pos[send_pos], jnp.zeros((), jnp.bfloat16))
    q_in = lax.all_to_all(q_out, "group", split_axis=0, concat_axis=0, tiled=True)
    q_rows = q_in[row_index]
    split = per_group // 2
    halves = ((slice(0, split), (0, 1)), (slice(split, per_group), (1, 0)))
    sums = []
    for rows_of, order in halves:
        q_all = torus_gather(q_rows[rows_of], grid, order)
        partial = attend_local(
            q_all, kv_cache[rows_of], row_live[rows_of], member_now * count, HEADS, jnp.bfloat16
        )
        sums.append(torus_reduce(partial, grid, order))
    summed = jnp.concatenate(sums, axis=0).astype(jnp.bfloat16)

    a_out = jnp.where(filled[:, None, None], summed[chosen], jnp.zeros((), summed.dtype))
    a_in = lax.all_to_all(a_out, "group", split_axis=0, concat_axis=0, tiled=True)
    attn = jnp.swapaxes(a_in[receive_index], 0, 1).astype(jnp.float32)

    gates = jax.nn.silu(jnp.dot(normed, w_uq[:, :width], preferred_element_type=jnp.float32))
    gates = gates.reshape(cand_rows, per_group, width)
    gated = (layer_norm(attn) * gates).astype(jnp.bfloat16).reshape(cand_rows * per_group, width)
    result = jnp.dot(gated, w_out, preferred_element_type=jnp.float32) + inputs.reshape(
        cand_rows * per_group, width
    )
    return result.astype(jnp.bfloat16).reshape(cand_rows, per_group, width)


def member_grid(mesh):
    members = mesh.shape["member"]
    try:
        line = mesh.devices[0]
        cols = len({d.coords[0] for d in line})
    except (AttributeError, TypeError, IndexError):
        cols = int(round(members ** 0.5))
    if cols < 1 or members % cols:
        cols = members
    return (members // cols, cols)


def solution(mesh):
    return jax.shard_map(
        functools.partial(on_device, member_grid(mesh)),
        mesh=mesh,
        in_specs=(P("member", "group", None), P("group", "member", None), P(), P(), P(), P(), P()),
        out_specs=P("member", "group", None),
        check_vma=False,
    )
```

```python
import functools

import jax
import jax.numpy as jnp
from jax import lax
from jax.experimental import pallas as pl
from jax.experimental.pallas import tpu as pltpu
from jax.sharding import PartitionSpec as P

HEADS = 8
BLK = 128


def layer_norm(values):
    center = values - jnp.mean(values, axis=-1, keepdims=True)
    spread = jnp.mean(center * center, axis=-1, keepdims=True)
    return center * lax.rsqrt(spread + 1e-05)


def routing(cache_request, rank_request, per_group):
    slot_ids = jnp.arange(cache_request.shape[0], dtype=jnp.int32)
    match = cache_request[:, None] == rank_request[None, :]
    rank_pos = jnp.sum(jnp.where(match, slot_ids[None, :], 0), axis=1)
    target = rank_pos // per_group
    owner_grp = slot_ids // per_group
    earlier = (
        (owner_grp[:, None] == owner_grp[None, :])
        & (target[:, None] == target[None, :])
        & (slot_ids[None, :] < slot_ids[:, None])
    )
    arrival = jnp.sum(earlier.astype(jnp.int32), axis=1)
    slot_of_pos = jnp.sum(jnp.where(match, slot_ids[:, None], 0), axis=0)
    return (target, arrival, slot_of_pos)


def attend_kernel(n_live_ref, q_ref, kv_ref, vk_ref, o_ref, *, heads, head_dim):
    row = pl.program_id(0)

    @pl.when(n_live_ref[row] <= 0)
    def _():
        o_ref[...] = jnp.zeros(o_ref.shape, o_ref.dtype)

    @pl.when(n_live_ref[row] > 0)
    def _():
        for h in range(heads):
            lo = h * head_dim
            q = q_ref[0, :, lo:lo + head_dim]
            k = kv_ref[0, :, lo:lo + head_dim]
            v = vk_ref[0, :, lo:lo + head_dim]
            t = lax.dot_general(q, k, (((1,), (1,)), ((), ())), preferred_element_type=jnp.float32)
            w = (t * (1.0 + jnp.tanh(t))).astype(jnp.bfloat16)
            o = jnp.dot(w, v, preferred_element_type=jnp.float32)
            o_ref[0, :, lo:lo + head_dim] = o.astype(o_ref.dtype)


def attend_local(queries, piece, live, first_event, heads, out_dtype):
    rows, cands, width = queries.shape
    count = piece.shape[1]
    head_dim = width // heads
    events = (first_event + jnp.arange(count)).astype(jnp.float32)
    keep = (events[None, :] < live[:, None]).astype(jnp.float32) / live[:, None]
    values = (piece[:, :, width:].astype(jnp.float32) * keep[:, :, None]).astype(jnp.bfloat16)
    n_live = jnp.clip(live.astype(jnp.int32) - first_event, 0, count).astype(jnp.int32)
    kernel = functools.partial(attend_kernel, heads=heads, head_dim=head_dim)
    flops = 4 * rows * cands * count * width
    return pl.pallas_call(
        kernel,
        out_shape=jax.ShapeDtypeStruct((rows, cands, width), out_dtype),
        grid_spec=pltpu.PrefetchScalarGridSpec(
            num_scalar_prefetch=1,
            grid=(rows,),
            in_specs=[
                pl.BlockSpec((1, cands, width), lambda r, n: (r, 0, 0)),
                pl.BlockSpec((1, count, width), lambda r, n: (r, 0, 0)),
                pl.BlockSpec((1, count, width), lambda r, n: (r, 0, 0)),
            ],
            out_specs=pl.BlockSpec((1, cands, width), lambda r, n: (r, 0, 0)),
        ),
        cost_estimate=pl.CostEstimate(
            flops=flops,
            transcendentals=rows * cands * count * heads,
            bytes_accessed=rows * (cands * width * 4 + count * width * 4),
        ),
    )(n_live, queries, piece, values)


def shift_perm(grid, axis, shift):
    rows, cols = grid
    pairs = []
    for zi in range(rows):
        for xi in range(cols):
            if axis == 0:
                dst = ((zi + shift) % rows) * cols + xi
            else:
                dst = zi * cols + (xi + shift) % cols
            pairs.append((zi * cols + xi, dst))
    return pairs


def send(value, grid, axis, shift):
    return lax.ppermute(value, "member", shift_perm(grid, axis, shift))


def ring_gather(block, grid, axis):
    n = grid[axis]
    slots = {0: block}
    ahead, behind = block, block
    for k in range(1, (n - 1) // 2 + 1):
        ahead = send(ahead, grid, axis, -1)
        behind = send(behind, grid, axis, 1)
        slots[k], slots[n - k] = ahead, behind
    if n % 2 == 0:
        if n == 2:
            slots[1] = send(block, grid, axis, -1)
        else:
            half = block.shape[1] // 2
            first = send(behind[:, :half], grid, axis, 1)
            second = send(ahead[:, half:], grid, axis, -1)
            slots[n // 2] = jnp.concatenate([first, second], axis=1)
    return jnp.concatenate([slots[r] for r in range(n)], axis=1)


def ring_reduce(parts, grid, axis):
    n = grid[axis]
    rows, total, width = parts.shape
    m = total // n
    slots = [parts[:, r * m:(r + 1) * m].astype(jnp.float32) for r in range(n)]
    if n == 1:
        return slots[0]
    if n == 2:
        return slots[0] + send(slots[1].astype(jnp.bfloat16), grid, axis, 1).astype(jnp.float32)
    top = (n - 1) // 2
    acc_ahead, acc_behind = slots[top], slots[n - top]
    if n % 2 == 0:
        half = m // 2
        far = slots[n // 2].astype(jnp.bfloat16)
        got_first = send(far[:, :half], grid, axis, 1).astype(jnp.float32)
        got_second = send(far[:, half:], grid, axis, -1).astype(jnp.float32)
        acc_ahead = acc_ahead + jnp.concatenate([got_first, jnp.zeros_like(got_first)], axis=1)
        acc_behind = acc_behind + jnp.concatenate([jnp.zeros_like(got_second), got_second], axis=1)
    for k in range(top, 0, -1):
        got_ahead = send(acc_ahead.astype(jnp.bfloat16), grid, axis, 1).astype(jnp.float32)
        got_behind = send(acc_behind.astype(jnp.bfloat16), grid, axis, -1).astype(jnp.float32)
        if k > 1:
            acc_ahead = slots[k - 1] + got_ahead
            acc_behind = slots[n - k + 1] + got_behind
        else:
            return slots[0] + got_ahead + got_behind


def torus_gather(block, grid, order):
    rows, m, width = block.shape
    out = ring_gather(block, grid, order[1])
    return ring_gather(out, grid, order[0])


def torus_reduce(parts, grid, order):
    out = ring_reduce(parts, grid, order[0])
    return ring_reduce(out, grid, order[1])


def on_device(grid, candidates, kv_cache, cache_request, rank_request, hist_blocks, w_uq, w_out):
    groups = lax.axis_size("group")
    per_group = kv_cache.shape[0]
    cand_rows = candidates.shape[0]
    width = candidates.shape[2]
    head_dim = width // HEADS
    count = kv_cache.shape[1]
    capacity = (per_group + groups - 1) // groups
    group_now = lax.axis_index("group")
    member_now = lax.axis_index("member")
    target, arrival, slot_of_pos = routing(cache_request, rank_request, per_group)
    first_slot = group_now * per_group
    local_target = lax.dynamic_slice_in_dim(target, first_slot, per_group)
    local_arrival = lax.dynamic_slice_in_dim(arrival, first_slot, per_group)
    row_index = local_target * capacity + local_arrival
    target_grid = jnp.arange(groups)[:, None, None]
    place_grid = jnp.arange(capacity)[None, :, None]
    hits = (local_target[None, None, :] == target_grid) & (
        local_arrival[None, None, :] == place_grid
    )
    chosen = jnp.sum(jnp.where(hits, jnp.arange(per_group)[None, None, :], 0), axis=2).reshape(-1)
    filled = jnp.any(hits, axis=2).reshape(-1)
    positions = first_slot + jnp.arange(per_group)
    source_slot = slot_of_pos[positions]
    receive_index = source_slot // per_group * capacity + arrival[source_slot]
    send_hits = receive_index[None, :] == jnp.arange(groups * capacity)[:, None]
    send_pos = jnp.sum(jnp.where(send_hits, jnp.arange(per_group)[None, :], 0), axis=1)
    send_filled = jnp.any(send_hits, axis=1)
    row_live = (hist_blocks[cache_request[first_slot + jnp.arange(per_group)]] * BLK).astype(
        jnp.float32
    )

    inputs = candidates.astype(jnp.float32)
    normed = layer_norm(inputs).astype(jnp.bfloat16).reshape(cand_rows * per_group, width)
    c_pos = jnp.swapaxes(candidates, 0, 1)
    c_out = jnp.where(send_filled[:, None, None], c_pos[send_pos], jnp.zeros((), candidates.dtype))
    c_in = lax.all_to_all(c_out, "group", split_axis=0, concat_axis=0, tiled=True)
    c_rows = c_in[row_index].reshape(-1, width)
    q_normed = layer_norm(c_rows.astype(jnp.float32)).astype(jnp.bfloat16)
    queries = jax.nn.silu(jnp.dot(q_normed, w_uq[:, width:], preferred_element_type=jnp.float32))
    q_rows = (queries * (0.5 * head_dim ** (-0.5))).astype(jnp.bfloat16).reshape(per_group, cand_rows, width)
    split = per_group // 2
    halves = ((slice(0, split), (0, 1)), (slice(split, per_group), (1, 0)))
    sums = []
    for rows_of, order in halves:
        q_all = torus_gather(q_rows[rows_of], grid, order)
        partial = attend_local(
            q_all, kv_cache[rows_of], row_live[rows_of], member_now * count, HEADS, jnp.bfloat16
        )
        sums.append(torus_reduce(partial, grid, order))
    summed = jnp.concatenate(sums, axis=0).astype(jnp.bfloat16)

    a_out = jnp.where(filled[:, None, None], summed[chosen], jnp.zeros((), summed.dtype))
    a_in = lax.all_to_all(a_out, "group", split_axis=0, concat_axis=0, tiled=True)
    attn = jnp.swapaxes(a_in[receive_index], 0, 1).astype(jnp.float32)

    gates = jax.nn.silu(jnp.dot(normed, w_uq[:, :width], preferred_element_type=jnp.float32))
    gates = gates.reshape(cand_rows, per_group, width)
    gated = (layer_norm(attn) * gates).astype(jnp.bfloat16).reshape(cand_rows * per_group, width)
    result = jnp.dot(gated, w_out, preferred_element_type=jnp.float32) + inputs.reshape(
        cand_rows * per_group, width
    )
    return result.astype(jnp.bfloat16).reshape(cand_rows, per_group, width)


def member_grid(mesh):
    members = mesh.shape["member"]
    try:
        line = mesh.devices[0]
        cols = len({d.coords[0] for d in line})
    except (AttributeError, TypeError, IndexError):
        cols = int(round(members ** 0.5))
    if cols < 1 or members % cols:
        cols = members
    return (members // cols, cols)


def solution(mesh):
    return jax.shard_map(
        functools.partial(on_device, member_grid(mesh)),
        mesh=mesh,
        in_specs=(P("member", "group", None), P("group", "member", None), P(), P(), P(), P(), P()),
        out_specs=P("member", "group", None),
        check_vma=False,
    )
```

```python
import functools

import jax
import jax.numpy as jnp
from jax import lax
from jax.experimental import pallas as pl
from jax.experimental.pallas import tpu as pltpu
from jax.sharding import PartitionSpec as P

HEADS = 8
BLK = 128


def layer_norm(values):
    center = values - jnp.mean(values, axis=-1, keepdims=True)
    spread = jnp.mean(center * center, axis=-1, keepdims=True)
    return center * lax.rsqrt(spread + 1e-05)


def routing(cache_request, rank_request, per_group):
    slot_ids = jnp.arange(cache_request.shape[0], dtype=jnp.int32)
    match = cache_request[:, None] == rank_request[None, :]
    rank_pos = jnp.sum(jnp.where(match, slot_ids[None, :], 0), axis=1)
    target = rank_pos // per_group
    owner_grp = slot_ids // per_group
    earlier = (
        (owner_grp[:, None] == owner_grp[None, :])
        & (target[:, None] == target[None, :])
        & (slot_ids[None, :] < slot_ids[:, None])
    )
    arrival = jnp.sum(earlier.astype(jnp.int32), axis=1)
    slot_of_pos = jnp.sum(jnp.where(match, slot_ids[:, None], 0), axis=0)
    return (target, arrival, slot_of_pos)


def attend_kernel(n_live_ref, q_ref, kv_ref, vk_ref, o_ref, *, heads, head_dim):
    row = pl.program_id(0)

    @pl.when(n_live_ref[row] <= 0)
    def _():
        o_ref[...] = jnp.zeros(o_ref.shape, o_ref.dtype)

    @pl.when(n_live_ref[row] > 0)
    def _():
        for h in range(heads):
            lo = h * head_dim
            q = q_ref[0, :, lo:lo + head_dim]
            k = kv_ref[0, :, lo:lo + head_dim]
            v = vk_ref[0, :, lo:lo + head_dim]
            t = lax.dot_general(q, k, (((1,), (1,)), ((), ())), preferred_element_type=jnp.float32)
            w = (t * (1.0 + jnp.tanh(t))).astype(jnp.bfloat16)
            o = jnp.dot(w, v, preferred_element_type=jnp.float32)
            o_ref[0, :, lo:lo + head_dim] = o.astype(o_ref.dtype)


def attend_local(queries, piece, live, first_event, heads, out_dtype):
    rows, cands, width = queries.shape
    count = piece.shape[1]
    head_dim = width // heads
    events = (first_event + jnp.arange(count)).astype(jnp.float32)
    keep = (events[None, :] < live[:, None]).astype(jnp.float32) / live[:, None]
    values = (piece[:, :, width:].astype(jnp.float32) * keep[:, :, None]).astype(jnp.bfloat16)
    n_live = jnp.clip(live.astype(jnp.int32) - first_event, 0, count).astype(jnp.int32)
    kernel = functools.partial(attend_kernel, heads=heads, head_dim=head_dim)
    flops = 4 * rows * cands * count * width
    return pl.pallas_call(
        kernel,
        out_shape=jax.ShapeDtypeStruct((rows, cands, width), out_dtype),
        grid_spec=pltpu.PrefetchScalarGridSpec(
            num_scalar_prefetch=1,
            grid=(rows,),
            in_specs=[
                pl.BlockSpec((1, cands, width), lambda r, n: (r, 0, 0)),
                pl.BlockSpec((1, count, width), lambda r, n: (r, 0, 0)),
                pl.BlockSpec((1, count, width), lambda r, n: (r, 0, 0)),
            ],
            out_specs=pl.BlockSpec((1, cands, width), lambda r, n: (r, 0, 0)),
        ),
        cost_estimate=pl.CostEstimate(
            flops=flops,
            transcendentals=rows * cands * count * heads,
            bytes_accessed=rows * (cands * width * 4 + count * width * 4),
        ),
    )(n_live, queries, piece, values)


def shift_perm(grid, axis, shift):
    rows, cols = grid
    pairs = []
    for zi in range(rows):
        for xi in range(cols):
            if axis == 0:
                dst = ((zi + shift) % rows) * cols + xi
            else:
                dst = zi * cols + (xi + shift) % cols
            pairs.append((zi * cols + xi, dst))
    return pairs


def send(value, grid, axis, shift):
    return lax.ppermute(value, "member", shift_perm(grid, axis, shift))


def ring_gather(block, grid, axis):
    n = grid[axis]
    slots = {0: block}
    ahead, behind = block, block
    for k in range(1, (n - 1) // 2 + 1):
        ahead = send(ahead, grid, axis, -1)
        behind = send(behind, grid, axis, 1)
        slots[k], slots[n - k] = ahead, behind
    if n % 2 == 0:
        if n == 2:
            slots[1] = send(block, grid, axis, -1)
        else:
            half = block.shape[1] // 2
            first = send(behind[:, :half], grid, axis, 1)
            second = send(ahead[:, half:], grid, axis, -1)
            slots[n // 2] = jnp.concatenate([first, second], axis=1)
    return jnp.concatenate([slots[r] for r in range(n)], axis=1)


def ring_reduce(parts, grid, axis):
    n = grid[axis]
    rows, total, width = parts.shape
    m = total // n
    slots = [parts[:, r * m:(r + 1) * m].astype(jnp.float32) for r in range(n)]
    if n == 1:
        return slots[0]
    if n == 2:
        return slots[0] + send(slots[1].astype(jnp.bfloat16), grid, axis, 1).astype(jnp.float32)
    top = (n - 1) // 2
    acc_ahead, acc_behind = slots[top], slots[n - top]
    if n % 2 == 0:
        half = m // 2
        far = slots[n // 2].astype(jnp.bfloat16)
        got_first = send(far[:, :half], grid, axis, 1).astype(jnp.float32)
        got_second = send(far[:, half:], grid, axis, -1).astype(jnp.float32)
        acc_ahead = acc_ahead + jnp.concatenate([got_first, jnp.zeros_like(got_first)], axis=1)
        acc_behind = acc_behind + jnp.concatenate([jnp.zeros_like(got_second), got_second], axis=1)
    for k in range(top, 0, -1):
        got_ahead = send(acc_ahead.astype(jnp.bfloat16), grid, axis, 1).astype(jnp.float32)
        got_behind = send(acc_behind.astype(jnp.bfloat16), grid, axis, -1).astype(jnp.float32)
        if k > 1:
            acc_ahead = slots[k - 1] + got_ahead
            acc_behind = slots[n - k + 1] + got_behind
        else:
            return slots[0] + got_ahead + got_behind


def torus_gather(block, grid, order):
    rows, m, width = block.shape
    out = ring_gather(block, grid, order[1])
    return ring_gather(out, grid, order[0])


def torus_reduce(parts, grid, order):
    out = ring_reduce(parts, grid, order[0])
    return ring_reduce(out, grid, order[1])


def on_device(grid, candidates, kv_cache, cache_request, rank_request, hist_blocks, w_uq, w_out):
    groups = lax.axis_size("group")
    per_group = kv_cache.shape[0]
    cand_rows = candidates.shape[0]
    width = candidates.shape[2]
    head_dim = width // HEADS
    count = kv_cache.shape[1]
    capacity = (per_group + groups - 1) // groups
    group_now = lax.axis_index("group")
    member_now = lax.axis_index("member")
    target, arrival, slot_of_pos = routing(cache_request, rank_request, per_group)
    first_slot = group_now * per_group
    local_target = lax.dynamic_slice_in_dim(target, first_slot, per_group)
    local_arrival = lax.dynamic_slice_in_dim(arrival, first_slot, per_group)
    row_index = local_target * capacity + local_arrival
    target_grid = jnp.arange(groups)[:, None, None]
    place_grid = jnp.arange(capacity)[None, :, None]
    hits = (local_target[None, None, :] == target_grid) & (
        local_arrival[None, None, :] == place_grid
    )
    chosen = jnp.sum(jnp.where(hits, jnp.arange(per_group)[None, None, :], 0), axis=2).reshape(-1)
    filled = jnp.any(hits, axis=2).reshape(-1)
    positions = first_slot + jnp.arange(per_group)
    source_slot = slot_of_pos[positions]
    receive_index = source_slot // per_group * capacity + arrival[source_slot]
    send_hits = receive_index[None, :] == jnp.arange(groups * capacity)[:, None]
    send_pos = jnp.sum(jnp.where(send_hits, jnp.arange(per_group)[None, :], 0), axis=1)
    send_filled = jnp.any(send_hits, axis=1)
    row_live = (hist_blocks[cache_request[first_slot + jnp.arange(per_group)]] * BLK).astype(
        jnp.float32
    )

    inputs = candidates.astype(jnp.float32)
    normed = layer_norm(inputs).astype(jnp.bfloat16).reshape(cand_rows * per_group, width)
    queries = jax.nn.silu(jnp.dot(normed, w_uq[:, width:], preferred_element_type=jnp.float32))
    queries = (queries * (0.5 * head_dim ** (-0.5))).astype(jnp.bfloat16).reshape(cand_rows, per_group, width)

    q_pos = jnp.swapaxes(queries, 0, 1)
    q_out = jnp.where(send_filled[:, None, None], q_pos[send_pos], jnp.zeros((), jnp.bfloat16))
    q_in = lax.all_to_all(q_out, "group", split_axis=0, concat_axis=0, tiled=True)
    q_rows = q_in[row_index]
    split = per_group // 2
    halves = ((slice(0, split), (0, 1)), (slice(split, per_group), (1, 0)))
    inner_first = ring_gather(q_rows[halves[0][0]], grid, halves[0][1][1])
    inner_first, rows_second = lax.optimization_barrier((inner_first, q_rows[halves[1][0]]))
    inner_second = ring_gather(rows_second, grid, halves[1][1][1])
    sums = []
    for (rows_of, order), inner in zip(halves, (inner_first, inner_second)):
        q_all = ring_gather(inner, grid, order[0])
        partial = attend_local(
            q_all, kv_cache[rows_of], row_live[rows_of], member_now * count, HEADS, jnp.bfloat16
        )
        sums.append(torus_reduce(partial, grid, order))
    summed = jnp.concatenate(sums, axis=0).astype(jnp.bfloat16)

    a_out = jnp.where(filled[:, None, None], summed[chosen], jnp.zeros((), summed.dtype))
    a_in = lax.all_to_all(a_out, "group", split_axis=0, concat_axis=0, tiled=True)
    attn = jnp.swapaxes(a_in[receive_index], 0, 1).astype(jnp.float32)

    gates = jax.nn.silu(jnp.dot(normed, w_uq[:, :width], preferred_element_type=jnp.float32))
    gates = gates.reshape(cand_rows, per_group, width)
    gated = (layer_norm(attn) * gates).astype(jnp.bfloat16).reshape(cand_rows * per_group, width)
    result = jnp.dot(gated, w_out, preferred_element_type=jnp.float32) + inputs.reshape(
        cand_rows * per_group, width
    )
    return result.astype(jnp.bfloat16).reshape(cand_rows, per_group, width)


def member_grid(mesh):
    members = mesh.shape["member"]
    try:
        line = mesh.devices[0]
        cols = len({d.coords[0] for d in line})
    except (AttributeError, TypeError, IndexError):
        cols = int(round(members ** 0.5))
    if cols < 1 or members % cols:
        cols = members
    return (members // cols, cols)


def solution(mesh):
    return jax.shard_map(
        functools.partial(on_device, member_grid(mesh)),
        mesh=mesh,
        in_specs=(P("member", "group", None), P("group", "member", None), P(), P(), P(), P(), P()),
        out_specs=P("member", "group", None),
        check_vma=False,
    )
```

```python
import functools

import jax
import jax.numpy as jnp
from jax import lax
from jax.experimental import pallas as pl
from jax.experimental.pallas import tpu as pltpu
from jax.sharding import PartitionSpec as P

HEADS = 8
BLK = 128


def layer_norm(values):
    center = values - jnp.mean(values, axis=-1, keepdims=True)
    spread = jnp.mean(center * center, axis=-1, keepdims=True)
    return center * lax.rsqrt(spread + 1e-05)


def routing(cache_request, rank_request, per_group):
    slot_ids = jnp.arange(cache_request.shape[0], dtype=jnp.int32)
    match = cache_request[:, None] == rank_request[None, :]
    rank_pos = jnp.sum(jnp.where(match, slot_ids[None, :], 0), axis=1)
    target = rank_pos // per_group
    owner_grp = slot_ids // per_group
    earlier = (
        (owner_grp[:, None] == owner_grp[None, :])
        & (target[:, None] == target[None, :])
        & (slot_ids[None, :] < slot_ids[:, None])
    )
    arrival = jnp.sum(earlier.astype(jnp.int32), axis=1)
    slot_of_pos = jnp.sum(jnp.where(match, slot_ids[:, None], 0), axis=0)
    return (target, arrival, slot_of_pos)


def attend_kernel(n_live_ref, *refs, sets, heads, head_dim):
    row = pl.program_id(0)
    rows = pl.num_programs(0)
    for j in range(sets):
        q_ref, kv_ref, vk_ref = refs[3 * j:3 * j + 3]
        o_ref = refs[3 * sets + j]
        live_here = n_live_ref[j * rows + row] > 0

        @pl.when(jnp.logical_not(live_here))
        def _():
            o_ref[...] = jnp.zeros(o_ref.shape, o_ref.dtype)

        @pl.when(live_here)
        def _():
            for h in range(heads):
                lo = h * head_dim
                q = q_ref[0, :, lo:lo + head_dim]
                k = kv_ref[0, :, lo:lo + head_dim]
                v = vk_ref[0, :, lo:lo + head_dim]
                t = lax.dot_general(q, k, (((1,), (1,)), ((), ())), preferred_element_type=jnp.float32)
                w = (t * (1.0 + jnp.tanh(t))).astype(jnp.bfloat16)
                o = jnp.dot(w, v, preferred_element_type=jnp.float32)
                o_ref[0, :, lo:lo + head_dim] = o.astype(o_ref.dtype)


def attend_local(q_sets, kv_sets, live_sets, first_event, heads, out_dtype):
    rows, cands, width = q_sets[0].shape
    count = kv_sets[0].shape[1]
    head_dim = width // heads
    events = (first_event + jnp.arange(count)).astype(jnp.float32)
    operands, n_live = [], []
    for queries, piece, live in zip(q_sets, kv_sets, live_sets):
        keep = (events[None, :] < live[:, None]).astype(jnp.float32) / live[:, None]
        values = (piece[:, :, width:].astype(jnp.float32) * keep[:, :, None]).astype(jnp.bfloat16)
        operands += [queries, piece, values]
        n_live.append(jnp.clip(live.astype(jnp.int32) - first_event, 0, count).astype(jnp.int32))
    sets = len(q_sets)
    kernel = functools.partial(attend_kernel, sets=sets, heads=heads, head_dim=head_dim)
    flops = 4 * sets * rows * cands * count * width
    set_specs = [
        pl.BlockSpec((1, cands, width), lambda r, n: (r, 0, 0)),
        pl.BlockSpec((1, count, width), lambda r, n: (r, 0, 0)),
        pl.BlockSpec((1, count, width), lambda r, n: (r, 0, 0)),
    ]
    return pl.pallas_call(
        kernel,
        out_shape=[jax.ShapeDtypeStruct((rows, cands, width), out_dtype) for _ in range(sets)],
        grid_spec=pltpu.PrefetchScalarGridSpec(
            num_scalar_prefetch=1,
            grid=(rows,),
            in_specs=set_specs * sets,
            out_specs=[pl.BlockSpec((1, cands, width), lambda r, n: (r, 0, 0)) for _ in range(sets)],
        ),
        cost_estimate=pl.CostEstimate(
            flops=flops,
            transcendentals=sets * rows * cands * count * heads,
            bytes_accessed=sets * rows * (cands * width * 4 + count * width * 4),
        ),
    )(jnp.concatenate(n_live), *operands)


def shift_perm(grid, axis, shift):
    rows, cols = grid
    pairs = []
    for zi in range(rows):
        for xi in range(cols):
            if axis == 0:
                dst = ((zi + shift) % rows) * cols + xi
            else:
                dst = zi * cols + (xi + shift) % cols
            pairs.append((zi * cols + xi, dst))
    return pairs


def send(value, grid, axis, shift):
    return lax.ppermute(value, "member", shift_perm(grid, axis, shift))


def ring_gather(block, grid, axis):
    n = grid[axis]
    slots = {0: block}
    ahead, behind = block, block
    for k in range(1, (n - 1) // 2 + 1):
        ahead = send(ahead, grid, axis, -1)
        behind = send(behind, grid, axis, 1)
        slots[k], slots[n - k] = ahead, behind
    if n % 2 == 0:
        if n == 2:
            slots[1] = send(block, grid, axis, -1)
        else:
            half = block.shape[1] // 2
            first = send(behind[:, :half], grid, axis, 1)
            second = send(ahead[:, half:], grid, axis, -1)
            slots[n // 2] = jnp.concatenate([first, second], axis=1)
    return jnp.concatenate([slots[r] for r in range(n)], axis=1)


def ring_reduce(parts, grid, axis):
    n = grid[axis]
    rows, total, width = parts.shape
    m = total // n
    slots = [parts[:, r * m:(r + 1) * m].astype(jnp.float32) for r in range(n)]
    if n == 1:
        return slots[0]
    if n == 2:
        return slots[0] + send(slots[1].astype(jnp.bfloat16), grid, axis, 1).astype(jnp.float32)
    top = (n - 1) // 2
    acc_ahead, acc_behind = slots[top], slots[n - top]
    if n % 2 == 0:
        half = m // 2
        far = slots[n // 2].astype(jnp.bfloat16)
        got_first = send(far[:, :half], grid, axis, 1).astype(jnp.float32)
        got_second = send(far[:, half:], grid, axis, -1).astype(jnp.float32)
        acc_ahead = acc_ahead + jnp.concatenate([got_first, jnp.zeros_like(got_first)], axis=1)
        acc_behind = acc_behind + jnp.concatenate([jnp.zeros_like(got_second), got_second], axis=1)
    for k in range(top, 0, -1):
        got_ahead = send(acc_ahead.astype(jnp.bfloat16), grid, axis, 1).astype(jnp.float32)
        got_behind = send(acc_behind.astype(jnp.bfloat16), grid, axis, -1).astype(jnp.float32)
        if k > 1:
            acc_ahead = slots[k - 1] + got_ahead
            acc_behind = slots[n - k + 1] + got_behind
        else:
            return slots[0] + got_ahead + got_behind


def torus_gather(block, grid, order):
    rows, m, width = block.shape
    out = ring_gather(block, grid, order[1])
    return ring_gather(out, grid, order[0])


def torus_reduce(parts, grid, order):
    out = ring_reduce(parts, grid, order[0])
    return ring_reduce(out, grid, order[1])


def on_device(grid, candidates, kv_cache, cache_request, rank_request, hist_blocks, w_uq, w_out):
    groups = lax.axis_size("group")
    per_group = kv_cache.shape[0]
    cand_rows = candidates.shape[0]
    width = candidates.shape[2]
    head_dim = width // HEADS
    count = kv_cache.shape[1]
    capacity = (per_group + groups - 1) // groups
    group_now = lax.axis_index("group")
    member_now = lax.axis_index("member")
    target, arrival, slot_of_pos = routing(cache_request, rank_request, per_group)
    first_slot = group_now * per_group
    local_target = lax.dynamic_slice_in_dim(target, first_slot, per_group)
    local_arrival = lax.dynamic_slice_in_dim(arrival, first_slot, per_group)
    row_index = local_target * capacity + local_arrival
    target_grid = jnp.arange(groups)[:, None, None]
    place_grid = jnp.arange(capacity)[None, :, None]
    hits = (local_target[None, None, :] == target_grid) & (
        local_arrival[None, None, :] == place_grid
    )
    chosen = jnp.sum(jnp.where(hits, jnp.arange(per_group)[None, None, :], 0), axis=2).reshape(-1)
    filled = jnp.any(hits, axis=2).reshape(-1)
    positions = first_slot + jnp.arange(per_group)
    source_slot = slot_of_pos[positions]
    receive_index = source_slot // per_group * capacity + arrival[source_slot]
    send_hits = receive_index[None, :] == jnp.arange(groups * capacity)[:, None]
    send_pos = jnp.sum(jnp.where(send_hits, jnp.arange(per_group)[None, :], 0), axis=1)
    send_filled = jnp.any(send_hits, axis=1)
    row_live = (hist_blocks[cache_request[first_slot + jnp.arange(per_group)]] * BLK).astype(
        jnp.float32
    )

    inputs = candidates.astype(jnp.float32)
    normed = layer_norm(inputs).astype(jnp.bfloat16).reshape(cand_rows * per_group, width)
    queries = jax.nn.silu(jnp.dot(normed, w_uq[:, width:], preferred_element_type=jnp.float32))
    queries = (queries * (0.5 * head_dim ** (-0.5))).astype(jnp.bfloat16).reshape(cand_rows, per_group, width)

    q_pos = jnp.swapaxes(queries, 0, 1)
    q_out = jnp.where(send_filled[:, None, None], q_pos[send_pos], jnp.zeros((), jnp.bfloat16))
    q_in = lax.all_to_all(q_out, "group", split_axis=0, concat_axis=0, tiled=True)
    q_rows = q_in[row_index]
    split = per_group // 2
    halves = ((slice(0, split), (0, 1)), (slice(split, per_group), (1, 0)))
    q_sets = [torus_gather(q_rows[rows_of], grid, order) for rows_of, order in halves]
    partials = attend_local(
        q_sets,
        [kv_cache[rows_of] for rows_of, _ in halves],
        [row_live[rows_of] for rows_of, _ in halves],
        member_now * count,
        HEADS,
        jnp.bfloat16,
    )
    sums = [torus_reduce(partial, grid, order) for partial, (_, order) in zip(partials, halves)]
    summed = jnp.concatenate(sums, axis=0).astype(jnp.bfloat16)

    a_out = jnp.where(filled[:, None, None], summed[chosen], jnp.zeros((), summed.dtype))
    a_in = lax.all_to_all(a_out, "group", split_axis=0, concat_axis=0, tiled=True)
    attn = jnp.swapaxes(a_in[receive_index], 0, 1).astype(jnp.float32)

    gates = jax.nn.silu(jnp.dot(normed, w_uq[:, :width], preferred_element_type=jnp.float32))
    gates = gates.reshape(cand_rows, per_group, width)
    gated = (layer_norm(attn) * gates).astype(jnp.bfloat16).reshape(cand_rows * per_group, width)
    result = jnp.dot(gated, w_out, preferred_element_type=jnp.float32) + inputs.reshape(
        cand_rows * per_group, width
    )
    return result.astype(jnp.bfloat16).reshape(cand_rows, per_group, width)


def member_grid(mesh):
    members = mesh.shape["member"]
    try:
        line = mesh.devices[0]
        cols = len({d.coords[0] for d in line})
    except (AttributeError, TypeError, IndexError):
        cols = int(round(members ** 0.5))
    if cols < 1 or members % cols:
        cols = members
    return (members // cols, cols)


def solution(mesh):
    return jax.shard_map(
        functools.partial(on_device, member_grid(mesh)),
        mesh=mesh,
        in_specs=(P("member", "group", None), P("group", "member", None), P(), P(), P(), P(), P()),
        out_specs=P("member", "group", None),
        check_vma=False,
    )
```

```python
import functools

import jax
import jax.numpy as jnp
from jax import lax
from jax.experimental import pallas as pl
from jax.experimental.pallas import tpu as pltpu
from jax.sharding import PartitionSpec as P

HEADS = 8
BLK = 128


def layer_norm(values):
    center = values - jnp.mean(values, axis=-1, keepdims=True)
    spread = jnp.mean(center * center, axis=-1, keepdims=True)
    return center * lax.rsqrt(spread + 1e-05)


def routing(cache_request, rank_request, per_group):
    slot_ids = jnp.arange(cache_request.shape[0], dtype=jnp.int32)
    match = cache_request[:, None] == rank_request[None, :]
    rank_pos = jnp.sum(jnp.where(match, slot_ids[None, :], 0), axis=1)
    target = rank_pos // per_group
    owner_grp = slot_ids // per_group
    earlier = (
        (owner_grp[:, None] == owner_grp[None, :])
        & (target[:, None] == target[None, :])
        & (slot_ids[None, :] < slot_ids[:, None])
    )
    arrival = jnp.sum(earlier.astype(jnp.int32), axis=1)
    slot_of_pos = jnp.sum(jnp.where(match, slot_ids[:, None], 0), axis=0)
    return (target, arrival, slot_of_pos)


def attend_kernel(n_live_ref, *refs, sets, heads, head_dim):
    row = pl.program_id(0)
    rows = pl.num_programs(0)
    for j in range(sets):
        q_ref, kv_ref, vk_ref = refs[3 * j:3 * j + 3]
        o_ref = refs[3 * sets + j]
        live_here = n_live_ref[j * rows + row] > 0

        @pl.when(jnp.logical_not(live_here))
        def _():
            o_ref[...] = jnp.zeros(o_ref.shape, o_ref.dtype)

        @pl.when(live_here)
        def _():
            for h in range(heads):
                lo = h * head_dim
                q = q_ref[0, :, lo:lo + head_dim]
                k = kv_ref[0, :, lo:lo + head_dim]
                v = vk_ref[0, :, lo:lo + head_dim]
                t = lax.dot_general(q, k, (((1,), (1,)), ((), ())), preferred_element_type=jnp.float32)
                w = (t * (1.0 + jnp.tanh(t))).astype(jnp.bfloat16)
                o = jnp.dot(w, v, preferred_element_type=jnp.float32)
                o_ref[0, :, lo:lo + head_dim] = o.astype(o_ref.dtype)


def attend_local(q_sets, kv_sets, live_sets, active_sets, first_event, heads, out_dtype):
    rows, cands, width = q_sets[0].shape
    count = kv_sets[0].shape[1]
    head_dim = width // heads
    events = (first_event + jnp.arange(count)).astype(jnp.float32)
    operands, n_live = [], []
    for queries, piece, live in zip(q_sets, kv_sets, live_sets):
        keep = (events[None, :] < live[:, None]).astype(jnp.float32) / live[:, None]
        values = (piece[:, :, width:].astype(jnp.float32) * keep[:, :, None]).astype(jnp.bfloat16)
        operands += [queries, piece, values]
        n_live.append(jnp.clip(live.astype(jnp.int32) - first_event, 0, count).astype(jnp.int32))
    n_live = [jnp.where(on, n, 0) for n, on in zip(n_live, active_sets)]
    sets = len(q_sets)
    kernel = functools.partial(attend_kernel, sets=sets, heads=heads, head_dim=head_dim)
    flops = 4 * sets * rows * cands * count * width
    set_specs = [
        pl.BlockSpec((1, cands, width), lambda r, n: (r, 0, 0)),
        pl.BlockSpec((1, count, width), lambda r, n: (r, 0, 0)),
        pl.BlockSpec((1, count, width), lambda r, n: (r, 0, 0)),
    ]
    return pl.pallas_call(
        kernel,
        out_shape=[jax.ShapeDtypeStruct((rows, cands, width), out_dtype) for _ in range(sets)],
        grid_spec=pltpu.PrefetchScalarGridSpec(
            num_scalar_prefetch=1,
            grid=(rows,),
            in_specs=set_specs * sets,
            out_specs=[pl.BlockSpec((1, cands, width), lambda r, n: (r, 0, 0)) for _ in range(sets)],
        ),
        cost_estimate=pl.CostEstimate(
            flops=flops,
            transcendentals=sets * rows * cands * count * heads,
            bytes_accessed=sets * rows * (cands * width * 4 + count * width * 4),
        ),
    )(jnp.concatenate(n_live), *operands)


def shift_perm(grid, axis, shift):
    rows, cols = grid
    pairs = []
    for zi in range(rows):
        for xi in range(cols):
            if axis == 0:
                dst = ((zi + shift) % rows) * cols + xi
            else:
                dst = zi * cols + (xi + shift) % cols
            pairs.append((zi * cols + xi, dst))
    return pairs


def send(value, grid, axis, shift):
    return lax.ppermute(value, "member", shift_perm(grid, axis, shift))


def ring_gather(block, grid, axis):
    n = grid[axis]
    slots = {0: block}
    ahead, behind = block, block
    for k in range(1, (n - 1) // 2 + 1):
        ahead = send(ahead, grid, axis, -1)
        behind = send(behind, grid, axis, 1)
        slots[k], slots[n - k] = ahead, behind
    if n % 2 == 0:
        if n == 2:
            slots[1] = send(block, grid, axis, -1)
        else:
            half = block.shape[1] // 2
            first = send(behind[:, :half], grid, axis, 1)
            second = send(ahead[:, half:], grid, axis, -1)
            slots[n // 2] = jnp.concatenate([first, second], axis=1)
    return jnp.concatenate([slots[r] for r in range(n)], axis=1)


def ring_reduce(parts, grid, axis):
    n = grid[axis]
    rows, total, width = parts.shape
    m = total // n
    slots = [parts[:, r * m:(r + 1) * m].astype(jnp.float32) for r in range(n)]
    if n == 1:
        return slots[0]
    if n == 2:
        return slots[0] + send(slots[1].astype(jnp.bfloat16), grid, axis, 1).astype(jnp.float32)
    top = (n - 1) // 2
    acc_ahead, acc_behind = slots[top], slots[n - top]
    if n % 2 == 0:
        half = m // 2
        far = slots[n // 2].astype(jnp.bfloat16)
        got_first = send(far[:, :half], grid, axis, 1).astype(jnp.float32)
        got_second = send(far[:, half:], grid, axis, -1).astype(jnp.float32)
        acc_ahead = acc_ahead + jnp.concatenate([got_first, jnp.zeros_like(got_first)], axis=1)
        acc_behind = acc_behind + jnp.concatenate([jnp.zeros_like(got_second), got_second], axis=1)
    for k in range(top, 0, -1):
        got_ahead = send(acc_ahead.astype(jnp.bfloat16), grid, axis, 1).astype(jnp.float32)
        got_behind = send(acc_behind.astype(jnp.bfloat16), grid, axis, -1).astype(jnp.float32)
        if k > 1:
            acc_ahead = slots[k - 1] + got_ahead
            acc_behind = slots[n - k + 1] + got_behind
        else:
            return slots[0] + got_ahead + got_behind


def torus_gather(block, grid, order):
    rows, m, width = block.shape
    out = ring_gather(block, grid, order[1])
    return ring_gather(out, grid, order[0])


def torus_reduce(parts, grid, order):
    out = ring_reduce(parts, grid, order[0])
    return ring_reduce(out, grid, order[1])


def on_device(grid, candidates, kv_cache, cache_request, rank_request, hist_blocks, w_uq, w_out):
    groups = lax.axis_size("group")
    per_group = kv_cache.shape[0]
    cand_rows = candidates.shape[0]
    width = candidates.shape[2]
    head_dim = width // HEADS
    count = kv_cache.shape[1]
    capacity = (per_group + groups - 1) // groups
    group_now = lax.axis_index("group")
    member_now = lax.axis_index("member")
    target, arrival, slot_of_pos = routing(cache_request, rank_request, per_group)
    first_slot = group_now * per_group
    local_target = lax.dynamic_slice_in_dim(target, first_slot, per_group)
    local_arrival = lax.dynamic_slice_in_dim(arrival, first_slot, per_group)
    row_index = local_target * capacity + local_arrival
    target_grid = jnp.arange(groups)[:, None, None]
    place_grid = jnp.arange(capacity)[None, :, None]
    hits = (local_target[None, None, :] == target_grid) & (
        local_arrival[None, None, :] == place_grid
    )
    chosen = jnp.sum(jnp.where(hits, jnp.arange(per_group)[None, None, :], 0), axis=2).reshape(-1)
    filled = jnp.any(hits, axis=2).reshape(-1)
    positions = first_slot + jnp.arange(per_group)
    source_slot = slot_of_pos[positions]
    receive_index = source_slot // per_group * capacity + arrival[source_slot]
    send_hits = receive_index[None, :] == jnp.arange(groups * capacity)[:, None]
    send_pos = jnp.sum(jnp.where(send_hits, jnp.arange(per_group)[None, :], 0), axis=1)
    send_filled = jnp.any(send_hits, axis=1)
    row_live = (hist_blocks[cache_request[first_slot + jnp.arange(per_group)]] * BLK).astype(
        jnp.float32
    )

    inputs = candidates.astype(jnp.float32)
    normed = layer_norm(inputs).astype(jnp.bfloat16).reshape(cand_rows * per_group, width)
    queries = jax.nn.silu(jnp.dot(normed, w_uq[:, width:], preferred_element_type=jnp.float32))
    queries = (queries * (0.5 * head_dim ** (-0.5))).astype(jnp.bfloat16).reshape(cand_rows, per_group, width)

    q_pos = jnp.swapaxes(queries, 0, 1)
    q_out = jnp.where(send_filled[:, None, None], q_pos[send_pos], jnp.zeros((), jnp.bfloat16))
    q_in = lax.all_to_all(q_out, "group", split_axis=0, concat_axis=0, tiled=True)
    kv_slots = kv_cache[chosen]
    live_slots = row_live[chosen]
    slot_count = q_in.shape[0]
    split = slot_count // 2
    halves = ((slice(0, split), (0, 1)), (slice(split, slot_count), (1, 0)))
    q_sets = [torus_gather(q_in[rows_of], grid, order) for rows_of, order in halves]
    partials = attend_local(
        q_sets,
        [kv_slots[rows_of] for rows_of, _ in halves],
        [live_slots[rows_of] for rows_of, _ in halves],
        [filled[rows_of] for rows_of, _ in halves],
        member_now * count,
        HEADS,
        jnp.bfloat16,
    )
    sums = [torus_reduce(partial, grid, order) for partial, (_, order) in zip(partials, halves)]
    summed = jnp.concatenate(sums, axis=0).astype(jnp.bfloat16)

    a_in = lax.all_to_all(summed, "group", split_axis=0, concat_axis=0, tiled=True)
    attn = jnp.swapaxes(a_in[receive_index], 0, 1).astype(jnp.float32)

    gates = jax.nn.silu(jnp.dot(normed, w_uq[:, :width], preferred_element_type=jnp.float32))
    gates = gates.reshape(cand_rows, per_group, width)
    gated = (layer_norm(attn) * gates).astype(jnp.bfloat16).reshape(cand_rows * per_group, width)
    result = jnp.dot(gated, w_out, preferred_element_type=jnp.float32) + inputs.reshape(
        cand_rows * per_group, width
    )
    return result.astype(jnp.bfloat16).reshape(cand_rows, per_group, width)


def member_grid(mesh):
    members = mesh.shape["member"]
    try:
        line = mesh.devices[0]
        cols = len({d.coords[0] for d in line})
    except (AttributeError, TypeError, IndexError):
        cols = int(round(members ** 0.5))
    if cols < 1 or members % cols:
        cols = members
    return (members // cols, cols)


def solution(mesh):
    return jax.shard_map(
        functools.partial(on_device, member_grid(mesh)),
        mesh=mesh,
        in_specs=(P("member", "group", None), P("group", "member", None), P(), P(), P(), P(), P()),
        out_specs=P("member", "group", None),
        check_vma=False,
    )
```

```python
import functools

import jax
import jax.numpy as jnp
from jax import lax
from jax.experimental import pallas as pl
from jax.experimental.pallas import tpu as pltpu
from jax.sharding import PartitionSpec as P

HEADS = 8
BLK = 128


def layer_norm(values):
    center = values - jnp.mean(values, axis=-1, keepdims=True)
    spread = jnp.mean(center * center, axis=-1, keepdims=True)
    return center * lax.rsqrt(spread + 1e-05)


def routing(cache_request, rank_request, per_group):
    slot_ids = jnp.arange(cache_request.shape[0], dtype=jnp.int32)
    match = cache_request[:, None] == rank_request[None, :]
    rank_pos = jnp.sum(jnp.where(match, slot_ids[None, :], 0), axis=1)
    target = rank_pos // per_group
    owner_grp = slot_ids // per_group
    earlier = (
        (owner_grp[:, None] == owner_grp[None, :])
        & (target[:, None] == target[None, :])
        & (slot_ids[None, :] < slot_ids[:, None])
    )
    arrival = jnp.sum(earlier.astype(jnp.int32), axis=1)
    slot_of_pos = jnp.sum(jnp.where(match, slot_ids[:, None], 0), axis=0)
    return (target, arrival, slot_of_pos)


def attend_kernel(n_live_ref, *refs, sets, heads, head_dim):
    row = pl.program_id(0)
    rows = pl.num_programs(0)
    for j in range(sets):
        q_ref, kv_ref, vk_ref = refs[3 * j:3 * j + 3]
        o_ref = refs[3 * sets + j]
        live_here = n_live_ref[j * rows + row] > 0

        @pl.when(jnp.logical_not(live_here))
        def _():
            o_ref[...] = jnp.zeros(o_ref.shape, o_ref.dtype)

        @pl.when(live_here)
        def _():
            for h in range(heads):
                lo = h * head_dim
                q = q_ref[0, :, lo:lo + head_dim]
                k = kv_ref[0, :, lo:lo + head_dim]
                v = vk_ref[0, :, lo:lo + head_dim]
                t = lax.dot_general(q, k, (((1,), (1,)), ((), ())), preferred_element_type=jnp.float32)
                w = (t * (1.0 + jnp.tanh(t))).astype(jnp.bfloat16)
                o = jnp.dot(w, v, preferred_element_type=jnp.float32)
                o_ref[0, :, lo:lo + head_dim] = o.astype(o_ref.dtype)


def attend_local(q_sets, kv_sets, live_sets, active_sets, first_event, heads, out_dtype):
    rows, cands, width = q_sets[0].shape
    count = kv_sets[0].shape[1]
    head_dim = width // heads
    events = (first_event + jnp.arange(count)).astype(jnp.float32)
    operands, n_live = [], []
    for queries, piece, live in zip(q_sets, kv_sets, live_sets):
        keep = (events[None, :] < live[:, None]).astype(jnp.float32) / live[:, None]
        values = (piece[:, :, width:].astype(jnp.float32) * keep[:, :, None]).astype(jnp.bfloat16)
        operands += [queries, piece, values]
        n_live.append(jnp.clip(live.astype(jnp.int32) - first_event, 0, count).astype(jnp.int32))
    n_live = [jnp.where(on, n, 0) for n, on in zip(n_live, active_sets)]
    sets = len(q_sets)
    kernel = functools.partial(attend_kernel, sets=sets, heads=heads, head_dim=head_dim)
    flops = 4 * sets * rows * cands * count * width
    set_specs = [
        pl.BlockSpec((1, cands, width), lambda r, n: (r, 0, 0)),
        pl.BlockSpec((1, count, width), lambda r, n: (r, 0, 0)),
        pl.BlockSpec((1, count, width), lambda r, n: (r, 0, 0)),
    ]
    return pl.pallas_call(
        kernel,
        out_shape=[jax.ShapeDtypeStruct((rows, cands, width), out_dtype) for _ in range(sets)],
        grid_spec=pltpu.PrefetchScalarGridSpec(
            num_scalar_prefetch=1,
            grid=(rows,),
            in_specs=set_specs * sets,
            out_specs=[pl.BlockSpec((1, cands, width), lambda r, n: (r, 0, 0)) for _ in range(sets)],
        ),
        cost_estimate=pl.CostEstimate(
            flops=flops,
            transcendentals=sets * rows * cands * count * heads,
            bytes_accessed=sets * rows * (cands * width * 4 + count * width * 4),
        ),
    )(jnp.concatenate(n_live), *operands)


def shift_perm(grid, axis, shift):
    rows, cols = grid
    pairs = []
    for zi in range(rows):
        for xi in range(cols):
            if axis == 0:
                dst = ((zi + shift) % rows) * cols + xi
            else:
                dst = zi * cols + (xi + shift) % cols
            pairs.append((zi * cols + xi, dst))
    return pairs


def send(value, grid, axis, shift):
    return lax.ppermute(value, "member", shift_perm(grid, axis, shift))


def ring_gather(block, grid, axis):
    n = grid[axis]
    slots = {0: block}
    ahead, behind = block, block
    for k in range(1, (n - 1) // 2 + 1):
        ahead = send(ahead, grid, axis, -1)
        behind = send(behind, grid, axis, 1)
        slots[k], slots[n - k] = ahead, behind
    if n % 2 == 0:
        if n == 2:
            slots[1] = send(block, grid, axis, -1)
        else:
            half = block.shape[1] // 2
            first = send(behind[:, :half], grid, axis, 1)
            second = send(ahead[:, half:], grid, axis, -1)
            slots[n // 2] = jnp.concatenate([first, second], axis=1)
    return jnp.concatenate([slots[r] for r in range(n)], axis=1)


def ring_reduce(parts, grid, axis):
    n = grid[axis]
    rows, total, width = parts.shape
    m = total // n
    slots = [parts[:, r * m:(r + 1) * m].astype(jnp.float32) for r in range(n)]
    if n == 1:
        return slots[0]
    if n == 2:
        return slots[0] + send(slots[1].astype(jnp.bfloat16), grid, axis, 1).astype(jnp.float32)
    top = (n - 1) // 2
    acc_ahead, acc_behind = slots[top], slots[n - top]
    if n % 2 == 0:
        half = m // 2
        far = slots[n // 2].astype(jnp.bfloat16)
        got_first = send(far[:, :half], grid, axis, 1).astype(jnp.float32)
        got_second = send(far[:, half:], grid, axis, -1).astype(jnp.float32)
        acc_ahead = acc_ahead + jnp.concatenate([got_first, jnp.zeros_like(got_first)], axis=1)
        acc_behind = acc_behind + jnp.concatenate([jnp.zeros_like(got_second), got_second], axis=1)
    for k in range(top, 0, -1):
        got_ahead = send(acc_ahead.astype(jnp.bfloat16), grid, axis, 1).astype(jnp.float32)
        got_behind = send(acc_behind.astype(jnp.bfloat16), grid, axis, -1).astype(jnp.float32)
        if k > 1:
            acc_ahead = slots[k - 1] + got_ahead
            acc_behind = slots[n - k + 1] + got_behind
        else:
            return slots[0] + got_ahead + got_behind


def torus_gather(block, grid, order):
    rows, m, width = block.shape
    out = ring_gather(block, grid, order[1])
    return ring_gather(out, grid, order[0])


def torus_reduce(parts, grid, order):
    out = ring_reduce(parts, grid, order[0])
    return ring_reduce(out, grid, order[1])


def on_device(grid, candidates, kv_cache, cache_request, rank_request, hist_blocks, w_uq, w_out):
    groups = lax.axis_size("group")
    per_group = kv_cache.shape[0]
    cand_rows = candidates.shape[0]
    width = candidates.shape[2]
    head_dim = width // HEADS
    count = kv_cache.shape[1]
    capacity = (per_group + groups - 1) // groups
    group_now = lax.axis_index("group")
    member_now = lax.axis_index("member")
    target, arrival, slot_of_pos = routing(cache_request, rank_request, per_group)
    first_slot = group_now * per_group
    local_target = lax.dynamic_slice_in_dim(target, first_slot, per_group)
    local_arrival = lax.dynamic_slice_in_dim(arrival, first_slot, per_group)
    row_index = local_target * capacity + local_arrival
    target_grid = jnp.arange(groups)[:, None, None]
    place_grid = jnp.arange(capacity)[None, :, None]
    hits = (local_target[None, None, :] == target_grid) & (
        local_arrival[None, None, :] == place_grid
    )
    chosen = jnp.sum(jnp.where(hits, jnp.arange(per_group)[None, None, :], 0), axis=2).reshape(-1)
    filled = jnp.any(hits, axis=2).reshape(-1)
    positions = first_slot + jnp.arange(per_group)
    source_slot = slot_of_pos[positions]
    receive_index = source_slot // per_group * capacity + arrival[source_slot]
    send_hits = receive_index[None, :] == jnp.arange(groups * capacity)[:, None]
    send_pos = jnp.sum(jnp.where(send_hits, jnp.arange(per_group)[None, :], 0), axis=1)
    send_filled = jnp.any(send_hits, axis=1)
    row_live = (hist_blocks[cache_request[first_slot + jnp.arange(per_group)]] * BLK).astype(
        jnp.float32
    )

    inputs = candidates.astype(jnp.float32)
    normed = layer_norm(inputs).astype(jnp.bfloat16).reshape(cand_rows * per_group, width)
    c_send = jnp.take(candidates, send_pos, axis=1)
    q_normed = layer_norm(c_send.astype(jnp.float32)).astype(jnp.bfloat16).reshape(-1, width)
    queries = jax.nn.silu(jnp.dot(q_normed, w_uq[:, width:], preferred_element_type=jnp.float32))
    queries = (queries * (0.5 * head_dim ** (-0.5))).astype(jnp.bfloat16).reshape(cand_rows, -1, width)

    q_out = jnp.where(send_filled[:, None, None], jnp.swapaxes(queries, 0, 1), jnp.zeros((), jnp.bfloat16))
    q_in = lax.all_to_all(q_out, "group", split_axis=0, concat_axis=0, tiled=True)
    kv_slots = kv_cache[chosen]
    live_slots = row_live[chosen]
    slot_count = q_in.shape[0]
    split = slot_count // 2
    halves = ((slice(0, split), (0, 1)), (slice(split, slot_count), (1, 0)))
    q_sets = [torus_gather(q_in[rows_of], grid, order) for rows_of, order in halves]
    partials = attend_local(
        q_sets,
        [kv_slots[rows_of] for rows_of, _ in halves],
        [live_slots[rows_of] for rows_of, _ in halves],
        [filled[rows_of] for rows_of, _ in halves],
        member_now * count,
        HEADS,
        jnp.bfloat16,
    )
    sums = [torus_reduce(partial, grid, order) for partial, (_, order) in zip(partials, halves)]
    summed = jnp.concatenate(sums, axis=0).astype(jnp.bfloat16)

    a_in = lax.all_to_all(summed, "group", split_axis=0, concat_axis=0, tiled=True)
    attn = jnp.swapaxes(a_in[receive_index], 0, 1).astype(jnp.float32)

    gates = jax.nn.silu(jnp.dot(normed, w_uq[:, :width], preferred_element_type=jnp.float32))
    gates = gates.reshape(cand_rows, per_group, width)
    gated = (layer_norm(attn) * gates).astype(jnp.bfloat16).reshape(cand_rows * per_group, width)
    result = jnp.dot(gated, w_out, preferred_element_type=jnp.float32) + inputs.reshape(
        cand_rows * per_group, width
    )
    return result.astype(jnp.bfloat16).reshape(cand_rows, per_group, width)


def member_grid(mesh):
    members = mesh.shape["member"]
    try:
        line = mesh.devices[0]
        cols = len({d.coords[0] for d in line})
    except (AttributeError, TypeError, IndexError):
        cols = int(round(members ** 0.5))
    if cols < 1 or members % cols:
        cols = members
    return (members // cols, cols)


def solution(mesh):
    return jax.shard_map(
        functools.partial(on_device, member_grid(mesh)),
        mesh=mesh,
        in_specs=(P("member", "group", None), P("group", "member", None), P(), P(), P(), P(), P()),
        out_specs=P("member", "group", None),
        check_vma=False,
    )
```

```python
import functools

import jax
import jax.numpy as jnp
from jax import lax
from jax.experimental import pallas as pl
from jax.experimental.pallas import tpu as pltpu
from jax.sharding import PartitionSpec as P

HEADS = 8
BLK = 128


def layer_norm(values):
    center = values - jnp.mean(values, axis=-1, keepdims=True)
    spread = jnp.mean(center * center, axis=-1, keepdims=True)
    return center * lax.rsqrt(spread + 1e-05)


def routing(cache_request, rank_request, per_group):
    slot_ids = jnp.arange(cache_request.shape[0], dtype=jnp.int32)
    match = cache_request[:, None] == rank_request[None, :]
    rank_pos = jnp.sum(jnp.where(match, slot_ids[None, :], 0), axis=1)
    target = rank_pos // per_group
    owner_grp = slot_ids // per_group
    earlier = (
        (owner_grp[:, None] == owner_grp[None, :])
        & (target[:, None] == target[None, :])
        & (slot_ids[None, :] < slot_ids[:, None])
    )
    arrival = jnp.sum(earlier.astype(jnp.int32), axis=1)
    slot_of_pos = jnp.sum(jnp.where(match, slot_ids[:, None], 0), axis=0)
    return (target, arrival, slot_of_pos)


def attend_kernel(n_live_ref, *refs, sets, heads, head_dim):
    row = pl.program_id(0)
    rows = pl.num_programs(0)
    for j in range(sets):
        q_ref, kv_ref, vk_ref = refs[3 * j:3 * j + 3]
        o_ref = refs[3 * sets + j]
        live_here = n_live_ref[j * rows + row] > 0

        @pl.when(jnp.logical_not(live_here))
        def _():
            o_ref[...] = jnp.zeros(o_ref.shape, o_ref.dtype)

        @pl.when(live_here)
        def _():
            for h in range(heads):
                lo = h * head_dim
                q = q_ref[0, :, lo:lo + head_dim]
                k = kv_ref[0, :, lo:lo + head_dim]
                v = vk_ref[0, :, lo:lo + head_dim]
                t = lax.dot_general(q, k, (((1,), (1,)), ((), ())), preferred_element_type=jnp.float32)
                w = (t * (1.0 + jnp.tanh(t))).astype(jnp.bfloat16)
                o = jnp.dot(w, v, preferred_element_type=jnp.float32)
                o_ref[0, :, lo:lo + head_dim] = o.astype(o_ref.dtype)


def masked_values(piece, live, first_event):
    count, width = piece.shape[1], piece.shape[2] // 2
    events = (first_event + jnp.arange(count)).astype(jnp.float32)
    keep = (events[None, :] < live[:, None]).astype(jnp.float32) / live[:, None]
    return (piece[:, :, width:].astype(jnp.float32) * keep[:, :, None]).astype(jnp.bfloat16)


def attend_local(q_sets, kv_sets, vk_sets, live_sets, active_sets, first_event, heads, out_dtype):
    rows, cands, width = q_sets[0].shape
    count = kv_sets[0].shape[1]
    head_dim = width // heads
    operands, n_live = [], []
    for queries, piece, values, live in zip(q_sets, kv_sets, vk_sets, live_sets):
        operands += [queries, piece, values]
        n_live.append(jnp.clip(live.astype(jnp.int32) - first_event, 0, count).astype(jnp.int32))
    n_live = [jnp.where(on, n, 0) for n, on in zip(n_live, active_sets)]
    sets = len(q_sets)
    kernel = functools.partial(attend_kernel, sets=sets, heads=heads, head_dim=head_dim)
    flops = 4 * sets * rows * cands * count * width
    set_specs = [
        pl.BlockSpec((1, cands, width), lambda r, n: (r, 0, 0)),
        pl.BlockSpec((1, count, width), lambda r, n: (r, 0, 0)),
        pl.BlockSpec((1, count, width), lambda r, n: (r, 0, 0)),
    ]
    return pl.pallas_call(
        kernel,
        out_shape=[jax.ShapeDtypeStruct((rows, cands, width), out_dtype) for _ in range(sets)],
        grid_spec=pltpu.PrefetchScalarGridSpec(
            num_scalar_prefetch=1,
            grid=(rows,),
            in_specs=set_specs * sets,
            out_specs=[pl.BlockSpec((1, cands, width), lambda r, n: (r, 0, 0)) for _ in range(sets)],
        ),
        cost_estimate=pl.CostEstimate(
            flops=flops,
            transcendentals=sets * rows * cands * count * heads,
            bytes_accessed=sets * rows * (cands * width * 4 + count * width * 4),
        ),
    )(jnp.concatenate(n_live), *operands)


def shift_perm(grid, axis, shift):
    rows, cols = grid
    pairs = []
    for zi in range(rows):
        for xi in range(cols):
            if axis == 0:
                dst = ((zi + shift) % rows) * cols + xi
            else:
                dst = zi * cols + (xi + shift) % cols
            pairs.append((zi * cols + xi, dst))
    return pairs


def send(value, grid, axis, shift):
    return lax.ppermute(value, "member", shift_perm(grid, axis, shift))


def ring_gather(block, grid, axis):
    n = grid[axis]
    slots = {0: block}
    ahead, behind = block, block
    for k in range(1, (n - 1) // 2 + 1):
        ahead = send(ahead, grid, axis, -1)
        behind = send(behind, grid, axis, 1)
        slots[k], slots[n - k] = ahead, behind
    if n % 2 == 0:
        if n == 2:
            slots[1] = send(block, grid, axis, -1)
        else:
            half = block.shape[1] // 2
            first = send(behind[:, :half], grid, axis, 1)
            second = send(ahead[:, half:], grid, axis, -1)
            slots[n // 2] = jnp.concatenate([first, second], axis=1)
    return jnp.concatenate([slots[r] for r in range(n)], axis=1)


def ring_reduce(parts, grid, axis):
    n = grid[axis]
    rows, total, width = parts.shape
    m = total // n
    slots = [parts[:, r * m:(r + 1) * m].astype(jnp.float32) for r in range(n)]
    if n == 1:
        return slots[0]
    if n == 2:
        return slots[0] + send(slots[1].astype(jnp.bfloat16), grid, axis, 1).astype(jnp.float32)
    top = (n - 1) // 2
    acc_ahead, acc_behind = slots[top], slots[n - top]
    if n % 2 == 0:
        half = m // 2
        far = slots[n // 2].astype(jnp.bfloat16)
        got_first = send(far[:, :half], grid, axis, 1).astype(jnp.float32)
        got_second = send(far[:, half:], grid, axis, -1).astype(jnp.float32)
        acc_ahead = acc_ahead + jnp.concatenate([got_first, jnp.zeros_like(got_first)], axis=1)
        acc_behind = acc_behind + jnp.concatenate([jnp.zeros_like(got_second), got_second], axis=1)
    for k in range(top, 0, -1):
        got_ahead = send(acc_ahead.astype(jnp.bfloat16), grid, axis, 1).astype(jnp.float32)
        got_behind = send(acc_behind.astype(jnp.bfloat16), grid, axis, -1).astype(jnp.float32)
        if k > 1:
            acc_ahead = slots[k - 1] + got_ahead
            acc_behind = slots[n - k + 1] + got_behind
        else:
            return slots[0] + got_ahead + got_behind


def torus_gather(block, grid, order):
    rows, m, width = block.shape
    out = ring_gather(block, grid, order[1])
    return ring_gather(out, grid, order[0])


def torus_reduce(parts, grid, order):
    out = ring_reduce(parts, grid, order[0])
    return ring_reduce(out, grid, order[1])


def on_device(grid, candidates, kv_cache, cache_request, rank_request, hist_blocks, w_uq, w_out):
    groups = lax.axis_size("group")
    per_group = kv_cache.shape[0]
    cand_rows = candidates.shape[0]
    width = candidates.shape[2]
    head_dim = width // HEADS
    count = kv_cache.shape[1]
    capacity = (per_group + groups - 1) // groups
    group_now = lax.axis_index("group")
    member_now = lax.axis_index("member")
    target, arrival, slot_of_pos = routing(cache_request, rank_request, per_group)
    first_slot = group_now * per_group
    local_target = lax.dynamic_slice_in_dim(target, first_slot, per_group)
    local_arrival = lax.dynamic_slice_in_dim(arrival, first_slot, per_group)
    row_index = local_target * capacity + local_arrival
    target_grid = jnp.arange(groups)[:, None, None]
    place_grid = jnp.arange(capacity)[None, :, None]
    hits = (local_target[None, None, :] == target_grid) & (
        local_arrival[None, None, :] == place_grid
    )
    chosen = jnp.sum(jnp.where(hits, jnp.arange(per_group)[None, None, :], 0), axis=2).reshape(-1)
    filled = jnp.any(hits, axis=2).reshape(-1)
    positions = first_slot + jnp.arange(per_group)
    source_slot = slot_of_pos[positions]
    receive_index = source_slot // per_group * capacity + arrival[source_slot]
    send_hits = receive_index[None, :] == jnp.arange(groups * capacity)[:, None]
    send_pos = jnp.sum(jnp.where(send_hits, jnp.arange(per_group)[None, :], 0), axis=1)
    send_filled = jnp.any(send_hits, axis=1)
    row_live = (hist_blocks[cache_request[first_slot + jnp.arange(per_group)]] * BLK).astype(
        jnp.float32
    )

    inputs = candidates.astype(jnp.float32)
    normed = layer_norm(inputs).astype(jnp.bfloat16).reshape(cand_rows * per_group, width)
    queries = jax.nn.silu(jnp.dot(normed, w_uq[:, width:], preferred_element_type=jnp.float32))
    queries = (queries * (0.5 * head_dim ** (-0.5))).astype(jnp.bfloat16).reshape(cand_rows, per_group, width)

    q_pos = jnp.swapaxes(queries, 0, 1)
    q_out = jnp.where(send_filled[:, None, None], q_pos[send_pos], jnp.zeros((), jnp.bfloat16))
    q_in = lax.all_to_all(q_out, "group", split_axis=0, concat_axis=0, tiled=True)
    kv_slots = kv_cache[chosen]
    vk_slots = masked_values(kv_cache, row_live, member_now * count)[chosen]
    live_slots = row_live[chosen]
    slot_count = q_in.shape[0]
    split = slot_count // 2
    halves = ((slice(0, split), (0, 1)), (slice(split, slot_count), (1, 0)))
    q_sets = [torus_gather(q_in[rows_of], grid, order) for rows_of, order in halves]
    partials = attend_local(
        q_sets,
        [kv_slots[rows_of] for rows_of, _ in halves],
        [vk_slots[rows_of] for rows_of, _ in halves],
        [live_slots[rows_of] for rows_of, _ in halves],
        [filled[rows_of] for rows_of, _ in halves],
        member_now * count,
        HEADS,
        jnp.bfloat16,
    )
    sums = [torus_reduce(partial, grid, order) for partial, (_, order) in zip(partials, halves)]
    summed = jnp.concatenate(sums, axis=0).astype(jnp.bfloat16)

    a_in = lax.all_to_all(summed, "group", split_axis=0, concat_axis=0, tiled=True)
    attn = jnp.swapaxes(a_in[receive_index], 0, 1).astype(jnp.float32)

    gates = jax.nn.silu(jnp.dot(normed, w_uq[:, :width], preferred_element_type=jnp.float32))
    gates = gates.reshape(cand_rows, per_group, width)
    gated = (layer_norm(attn) * gates).astype(jnp.bfloat16).reshape(cand_rows * per_group, width)
    result = jnp.dot(gated, w_out, preferred_element_type=jnp.float32) + inputs.reshape(
        cand_rows * per_group, width
    )
    return result.astype(jnp.bfloat16).reshape(cand_rows, per_group, width)


def member_grid(mesh):
    members = mesh.shape["member"]
    try:
        line = mesh.devices[0]
        cols = len({d.coords[0] for d in line})
    except (AttributeError, TypeError, IndexError):
        cols = int(round(members ** 0.5))
    if cols < 1 or members % cols:
        cols = members
    return (members // cols, cols)


def solution(mesh):
    return jax.shard_map(
        functools.partial(on_device, member_grid(mesh)),
        mesh=mesh,
        in_specs=(P("member", "group", None), P("group", "member", None), P(), P(), P(), P(), P()),
        out_specs=P("member", "group", None),
        check_vma=False,
    )
```

```python
import functools

import jax
import jax.numpy as jnp
from jax import lax
from jax.experimental import pallas as pl
from jax.experimental.pallas import tpu as pltpu
from jax.sharding import PartitionSpec as P

HEADS = 8
BLK = 128


def layer_norm(values):
    center = values - jnp.mean(values, axis=-1, keepdims=True)
    spread = jnp.mean(center * center, axis=-1, keepdims=True)
    return center * lax.rsqrt(spread + 1e-05)


def routing(cache_request, rank_request, per_group):
    slot_ids = jnp.arange(cache_request.shape[0], dtype=jnp.int32)
    match = cache_request[:, None] == rank_request[None, :]
    rank_pos = jnp.sum(jnp.where(match, slot_ids[None, :], 0), axis=1)
    target = rank_pos // per_group
    owner_grp = slot_ids // per_group
    earlier = (
        (owner_grp[:, None] == owner_grp[None, :])
        & (target[:, None] == target[None, :])
        & (slot_ids[None, :] < slot_ids[:, None])
    )
    arrival = jnp.sum(earlier.astype(jnp.int32), axis=1)
    slot_of_pos = jnp.sum(jnp.where(match, slot_ids[:, None], 0), axis=0)
    return (target, arrival, slot_of_pos)


def attend_kernel(n_live_ref, *refs, sets, heads, head_dim):
    row = pl.program_id(0)
    rows = pl.num_programs(0)
    for j in range(sets):
        q_ref, kv_ref, vk_ref = refs[3 * j:3 * j + 3]
        o_ref = refs[3 * sets + j]
        live_here = n_live_ref[j * rows + row] > 0

        @pl.when(jnp.logical_not(live_here))
        def _():
            o_ref[...] = jnp.zeros(o_ref.shape, o_ref.dtype)

        @pl.when(live_here)
        def _():
            for h in range(heads):
                lo = h * head_dim
                q = q_ref[0, :, lo:lo + head_dim]
                k = kv_ref[0, :, lo:lo + head_dim]
                v = vk_ref[0, :, lo:lo + head_dim]
                t = lax.dot_general(q, k, (((1,), (1,)), ((), ())), preferred_element_type=jnp.float32)
                w = (t * (1.0 + jnp.tanh(t))).astype(jnp.bfloat16)
                o = jnp.dot(w, v, preferred_element_type=jnp.float32)
                o_ref[0, :, lo:lo + head_dim] = o.astype(o_ref.dtype)


def attend_local(q_sets, kv_sets, live_sets, active_sets, first_event, heads, out_dtype):
    rows, cands, width = q_sets[0].shape
    count = kv_sets[0].shape[1]
    head_dim = width // heads
    events = (first_event + jnp.arange(count)).astype(jnp.float32)
    operands, n_live = [], []
    for queries, piece, live in zip(q_sets, kv_sets, live_sets):
        keep = (events[None, :] < live[:, None]).astype(jnp.float32) / live[:, None]
        values = (piece[:, :, width:].astype(jnp.float32) * keep[:, :, None]).astype(jnp.bfloat16)
        operands += [queries, piece, values]
        n_live.append(jnp.clip(live.astype(jnp.int32) - first_event, 0, count).astype(jnp.int32))
    n_live = [jnp.where(on, n, 0) for n, on in zip(n_live, active_sets)]
    sets = len(q_sets)
    kernel = functools.partial(attend_kernel, sets=sets, heads=heads, head_dim=head_dim)
    flops = 4 * sets * rows * cands * count * width
    set_specs = [
        pl.BlockSpec((1, cands, width), lambda r, n: (r, 0, 0)),
        pl.BlockSpec((1, count, width), lambda r, n: (r, 0, 0)),
        pl.BlockSpec((1, count, width), lambda r, n: (r, 0, 0)),
    ]
    return pl.pallas_call(
        kernel,
        out_shape=[jax.ShapeDtypeStruct((rows, cands, width), out_dtype) for _ in range(sets)],
        grid_spec=pltpu.PrefetchScalarGridSpec(
            num_scalar_prefetch=1,
            grid=(rows,),
            in_specs=set_specs * sets,
            out_specs=[pl.BlockSpec((1, cands, width), lambda r, n: (r, 0, 0)) for _ in range(sets)],
        ),
        cost_estimate=pl.CostEstimate(
            flops=flops,
            transcendentals=sets * rows * cands * count * heads,
            bytes_accessed=sets * rows * (cands * width * 4 + count * width * 4),
        ),
    )(jnp.concatenate(n_live), *operands)


def shift_perm(grid, axis, shift):
    rows, cols = grid
    pairs = []
    for zi in range(rows):
        for xi in range(cols):
            if axis == 0:
                dst = ((zi + shift) % rows) * cols + xi
            else:
                dst = zi * cols + (xi + shift) % cols
            pairs.append((zi * cols + xi, dst))
    return pairs


def send(value, grid, axis, shift):
    return lax.ppermute(value, "member", shift_perm(grid, axis, shift))


def ring_gather(block, grid, axis, split_far=True):
    n = grid[axis]
    slots = {0: block}
    ahead, behind = block, block
    for k in range(1, (n - 1) // 2 + 1):
        ahead = send(ahead, grid, axis, -1)
        behind = send(behind, grid, axis, 1)
        slots[k], slots[n - k] = ahead, behind
    if n % 2 == 0:
        if n == 2:
            slots[1] = send(block, grid, axis, -1)
        elif not split_far:
            slots[n // 2] = send(behind, grid, axis, 1)
        else:
            half = block.shape[1] // 2
            first = send(behind[:, :half], grid, axis, 1)
            second = send(ahead[:, half:], grid, axis, -1)
            slots[n // 2] = jnp.concatenate([first, second], axis=1)
    return jnp.concatenate([slots[r] for r in range(n)], axis=1)


def ring_reduce(parts, grid, axis, split_far=True):
    n = grid[axis]
    rows, total, width = parts.shape
    m = total // n
    slots = [parts[:, r * m:(r + 1) * m].astype(jnp.float32) for r in range(n)]
    if n == 1:
        return slots[0]
    if n == 2:
        return slots[0] + send(slots[1].astype(jnp.bfloat16), grid, axis, 1).astype(jnp.float32)
    top = (n - 1) // 2
    acc_ahead, acc_behind = slots[top], slots[n - top]
    if n % 2 == 0 and not split_far:
        acc_ahead = acc_ahead + send(slots[n // 2].astype(jnp.bfloat16), grid, axis, 1).astype(jnp.float32)
    elif n % 2 == 0:
        half = m // 2
        far = slots[n // 2].astype(jnp.bfloat16)
        got_first = send(far[:, :half], grid, axis, 1).astype(jnp.float32)
        got_second = send(far[:, half:], grid, axis, -1).astype(jnp.float32)
        acc_ahead = acc_ahead + jnp.concatenate([got_first, jnp.zeros_like(got_first)], axis=1)
        acc_behind = acc_behind + jnp.concatenate([jnp.zeros_like(got_second), got_second], axis=1)
    for k in range(top, 0, -1):
        got_ahead = send(acc_ahead.astype(jnp.bfloat16), grid, axis, 1).astype(jnp.float32)
        got_behind = send(acc_behind.astype(jnp.bfloat16), grid, axis, -1).astype(jnp.float32)
        if k > 1:
            acc_ahead = slots[k - 1] + got_ahead
            acc_behind = slots[n - k + 1] + got_behind
        else:
            return slots[0] + got_ahead + got_behind


def torus_gather(block, grid, order):
    rows, m, width = block.shape
    out = ring_gather(block, grid, order[1], split_far=False)
    return ring_gather(out, grid, order[0])


def torus_reduce(parts, grid, order):
    out = ring_reduce(parts, grid, order[0])
    return ring_reduce(out, grid, order[1], split_far=False)


def on_device(grid, candidates, kv_cache, cache_request, rank_request, hist_blocks, w_uq, w_out):
    groups = lax.axis_size("group")
    per_group = kv_cache.shape[0]
    cand_rows = candidates.shape[0]
    width = candidates.shape[2]
    head_dim = width // HEADS
    count = kv_cache.shape[1]
    capacity = (per_group + groups - 1) // groups
    group_now = lax.axis_index("group")
    member_now = lax.axis_index("member")
    target, arrival, slot_of_pos = routing(cache_request, rank_request, per_group)
    first_slot = group_now * per_group
    local_target = lax.dynamic_slice_in_dim(target, first_slot, per_group)
    local_arrival = lax.dynamic_slice_in_dim(arrival, first_slot, per_group)
    row_index = local_target * capacity + local_arrival
    target_grid = jnp.arange(groups)[:, None, None]
    place_grid = jnp.arange(capacity)[None, :, None]
    hits = (local_target[None, None, :] == target_grid) & (
        local_arrival[None, None, :] == place_grid
    )
    chosen = jnp.sum(jnp.where(hits, jnp.arange(per_group)[None, None, :], 0), axis=2).reshape(-1)
    filled = jnp.any(hits, axis=2).reshape(-1)
    positions = first_slot + jnp.arange(per_group)
    source_slot = slot_of_pos[positions]
    receive_index = source_slot // per_group * capacity + arrival[source_slot]
    send_hits = receive_index[None, :] == jnp.arange(groups * capacity)[:, None]
    send_pos = jnp.sum(jnp.where(send_hits, jnp.arange(per_group)[None, :], 0), axis=1)
    send_filled = jnp.any(send_hits, axis=1)
    row_live = (hist_blocks[cache_request[first_slot + jnp.arange(per_group)]] * BLK).astype(
        jnp.float32
    )

    inputs = candidates.astype(jnp.float32)
    normed = layer_norm(inputs).astype(jnp.bfloat16).reshape(cand_rows * per_group, width)
    queries = jax.nn.silu(jnp.dot(normed, w_uq[:, width:], preferred_element_type=jnp.float32))
    queries = (queries * (0.5 * head_dim ** (-0.5))).astype(jnp.bfloat16).reshape(cand_rows, per_group, width)

    q_pos = jnp.swapaxes(queries, 0, 1)
    q_out = jnp.where(send_filled[:, None, None], q_pos[send_pos], jnp.zeros((), jnp.bfloat16))
    q_in = lax.all_to_all(q_out, "group", split_axis=0, concat_axis=0, tiled=True)
    kv_slots = kv_cache[chosen]
    live_slots = row_live[chosen]
    slot_count = q_in.shape[0]
    split = slot_count // 2
    halves = ((slice(0, split), (0, 1)), (slice(split, slot_count), (1, 0)))
    q_sets = [torus_gather(q_in[rows_of], grid, order) for rows_of, order in halves]
    partials = attend_local(
        q_sets,
        [kv_slots[rows_of] for rows_of, _ in halves],
        [live_slots[rows_of] for rows_of, _ in halves],
        [filled[rows_of] for rows_of, _ in halves],
        member_now * count,
        HEADS,
        jnp.bfloat16,
    )
    sums = [torus_reduce(partial, grid, order) for partial, (_, order) in zip(partials, halves)]
    summed = jnp.concatenate(sums, axis=0).astype(jnp.bfloat16)

    a_in = lax.all_to_all(summed, "group", split_axis=0, concat_axis=0, tiled=True)
    attn = jnp.swapaxes(a_in[receive_index], 0, 1).astype(jnp.float32)

    gates = jax.nn.silu(jnp.dot(normed, w_uq[:, :width], preferred_element_type=jnp.float32))
    gates = gates.reshape(cand_rows, per_group, width)
    gated = (layer_norm(attn) * gates).astype(jnp.bfloat16).reshape(cand_rows * per_group, width)
    result = jnp.dot(gated, w_out, preferred_element_type=jnp.float32) + inputs.reshape(
        cand_rows * per_group, width
    )
    return result.astype(jnp.bfloat16).reshape(cand_rows, per_group, width)


def member_grid(mesh):
    members = mesh.shape["member"]
    try:
        line = mesh.devices[0]
        cols = len({d.coords[0] for d in line})
    except (AttributeError, TypeError, IndexError):
        cols = int(round(members ** 0.5))
    if cols < 1 or members % cols:
        cols = members
    return (members // cols, cols)


def solution(mesh):
    return jax.shard_map(
        functools.partial(on_device, member_grid(mesh)),
        mesh=mesh,
        in_specs=(P("member", "group", None), P("group", "member", None), P(), P(), P(), P(), P()),
        out_specs=P("member", "group", None),
        check_vma=False,
    )
```
